32 devices in a mesh: seq: 8 (over y, x, core), fsdp: 4 (over z).
Axes of the slice: x: 2, y: 2, z: 4, core: 2. Of those that a mesh axis runs over, the one named last changes fastest.
Arguments:
- tokens: bfloat16 [4, 4096, 3072], P('fsdp', 'seq'), may hold values from -6 to 6
- doc_ids: int32 [4, 4096], P('fsdp', 'seq'), may hold values from 0 to 15, never falling along the last dimension, each value on 1 to 1024 neighbouring positions
- norm_gain: float32 [3072], replicated, may hold values from 0.5 to 2
- query_weight: bfloat16 [3072, 1536], P(('seq', 'fsdp')), may hold values from -0.109375 to 0.109375
- key_weight: bfloat16 [3072, 1536], P(('seq', 'fsdp')), may hold values from -0.109375 to 0.109375
- value_weight: bfloat16 [3072, 1536], P(('seq', 'fsdp')), may hold values from -0.109375 to 0.109375
- out_gain: float32 [1536], replicated, may hold values from 0.5 to 2
Outputs:
- attended: bfloat16 [4, 4096, 1536], P('fsdp', 'seq')
The draws below stay inside these ranges and needn't reach their ends.
Inputs may be any that keep to these rules, and one draw needn't show every extreme that they name: `doc_ids`: document numbers never fall along a stream, so every document is one run of consecutive tokens; every number below 16 is used in each stream, every run holds at most 1024 tokens, and one run holds exactly 1024.
All inputs are finite; a program needn't handle non-finite values.
Results may differ from the reference program's by a relative error of at most 0.0044.
Values may be sent and summed in bfloat16 or wider, within the bound.
No kernel may reach another device: no remote copies, remote signals or barrier semaphores. Data moves between devices by JAX's collectives and lax.ppermute only.
A program may use at most 128 MiB of HBM per device.

```python
import math
import jax
import jax.numpy as jnp
import numpy as np
from jax import lax

D = 3072
HEADS = 12
HEAD_DIM = 128
TOK_DEV = 512
ATTN_WIDTH = 1536
STREAMS = 4
STREAM = 4096
DOCS = 16
MOST = 1024
N_SEQ = 8


def steps_of(key, shape, pieces, smallest, largest):
    loudness, own = 1.0, jax.random.fold_in(key, 6)
    for dim, parts in pieces:
        steps = jnp.exp(jax.random.uniform(jax.random.fold_in(own, dim), (parts,), jnp.float32, smallest / len(pieces), largest / len(pieces)))
        loudness = loudness * jnp.repeat(steps, shape[dim] // parts).reshape([-1 if axis == dim else 1 for axis in range(len(shape))])
    return loudness


def profile(amount, total, bound, slope):
    weights = [(1 << 20) // math.isqrt(standing ** slope) + 1 for standing in range(2, amount + 1)]
    surplus, given = total - bound - (amount - 1), [1] * (amount - 1)
    while surplus > 0:
        movable = [i for i in range(amount - 1) if given[i] < bound]
        whole, left = sum([weights[i] for i in movable]), surplus
        for i in movable:
            extra = min(bound - given[i], max(1, left * weights[i] // whole), surplus)
            given[i] = given[i] + extra
            surplus = surplus - extra
    return np.array([bound] + given)


def ragged_sizes(rng, amount, total, bound, skew):
    if amount == 2:
        one = jax.random.randint(rng, (), max(1, total - bound), min(bound, total - 1) + 1)
        return jnp.stack([one, total - one])
    tallies = jnp.asarray(profile(amount, total, bound, skew), jnp.int32)
    couples = (amount - 1) // 2
    donor, sink = tallies[1:1 + 2 * couples:2], tallies[2:2 + 2 * couples:2]
    margin = jnp.minimum(donor - 1, bound - sink)
    moved = jax.random.randint(jax.random.fold_in(rng, 1), (couples,), 0, 1 << 20) % (margin + 1)
    tallies = tallies.at[1:1 + 2 * couples:2].set(donor - moved).at[2:2 + 2 * couples:2].set(sink + moved)
    return tallies[jax.random.permutation(jax.random.fold_in(rng, 2), amount)]


def noise(rng, shape, scale, most, shards=(), dtype=jnp.bfloat16):
    level = steps_of(rng, shape, shards, -0.22, 0.18) if shards else 1.0
    result = jax.random.normal(rng, shape, jnp.float32) * scale * level
    return jnp.minimum(jnp.maximum(result, -most), most).astype(dtype)


def setup_inputs(seed: int = 0) -> dict:
    key_of = jax.random.split(jax.random.key(seed), 8)
    tokens = noise(key_of[0], (STREAMS, STREAM, D), 1.0, 6.0, ((0, 4), (1, 8)))
    doc_ids = jax.vmap(lambda own: jnp.searchsorted(jnp.cumsum(ragged_sizes(own, DOCS, STREAM, MOST, 2)), jnp.arange(STREAM), side="right"))(jax.random.split(key_of[1], STREAMS)).reshape((STREAMS, STREAM)).astype(jnp.int32)
    norm_gain = jnp.clip(jnp.exp(jax.random.uniform(key_of[2], (D,), jnp.float32, math.log(0.5), math.log(2.0))), 0.5, 2.0)
    query_weight = noise(key_of[3], (D, ATTN_WIDTH), D ** -0.5, 0.109375, ((0, 32),))
    key_weight = noise(key_of[4], (D, ATTN_WIDTH), D ** -0.5, 0.109375, ((0, 32),))
    value_weight = noise(key_of[5], (D, ATTN_WIDTH), D ** -0.5, 0.109375, ((0, 32),))
    out_gain = jnp.clip(jnp.exp(jax.random.uniform(key_of[6], (ATTN_WIDTH,), jnp.float32, math.log(0.5), math.log(2.0))), 0.5, 2.0)
    return dict(tokens=tokens, doc_ids=doc_ids, norm_gain=norm_gain, query_weight=query_weight, key_weight=key_weight, value_weight=value_weight, out_gain=out_gain)


EPS = 1e-06

def round_trip(values):
    return lax.optimization_barrier(values.astype(jnp.bfloat16)).astype(jnp.float32)

def norm_rows(values, gain):
    mean_sq = lax.optimization_barrier(jnp.mean(values * values, axis=-1, keepdims=True))
    return values * lax.rsqrt(mean_sq + EPS) * gain

def block_mix(query_rows, key_rows, value_rows, doc_block, carried, carried_doc):
    count = doc_block.shape[0]
    scores = jnp.einsum('ihe,jhe->hij', query_rows, key_rows)
    positions = jnp.arange(count)
    visible = (positions[:, None] >= positions[None, :]) & (doc_block[:, None] == doc_block[None, :])
    weights = round_trip(jnp.where(visible[None], scores, 0.0))
    local_part = jnp.einsum('hij,jhe->ihe', weights, value_rows)
    carried_low = round_trip(carried)
    from_past = jnp.einsum('ihe,hef->ihf', query_rows, carried_low)
    joined = (doc_block == carried_doc)[:, None, None]
    mixed = local_part + jnp.where(joined, from_past, 0.0)
    last_doc = doc_block[-1]
    tail_keys = jnp.where((doc_block == last_doc)[:, None, None], key_rows, 0.0)
    tail_state = jnp.einsum('jhe,jhf->hef', tail_keys, value_rows)
    return (mixed, tail_state)

def reference(tokens, doc_ids, norm_gain, query_weight, key_weight, value_weight, out_gain):
    query_wide = query_weight.astype(jnp.float32)
    key_wide = key_weight.astype(jnp.float32)
    value_wide = value_weight.astype(jnp.float32)

    def project(normed, weight):
        product = jnp.dot(normed, weight, precision=lax.Precision.HIGHEST)
        return round_trip(jax.nn.silu(product)).reshape(TOK_DEV, HEADS, HEAD_DIM)

    def one_stream(stream_pair):
        stream_tokens, stream_docs = stream_pair
        blocks = stream_tokens.reshape(N_SEQ, TOK_DEV, D)
        doc_blocks = stream_docs.reshape(N_SEQ, TOK_DEV)

        def advance(carry_pair, block_pair):
            carried, carried_doc = carry_pair
            block_tokens, doc_block = block_pair
            normed = round_trip(norm_rows(block_tokens.astype(jnp.float32), norm_gain.astype(jnp.float32)))
            query_rows = project(normed, query_wide)
            key_rows = project(normed, key_wide)
            value_rows = project(normed, value_wide)
            mixed, tail_state = block_mix(query_rows, key_rows, value_rows, doc_block, carried, carried_doc)
            continues = (doc_block[0] == carried_doc) & (doc_block[0] == doc_block[-1])
            new_state = tail_state + jnp.where(continues, carried, 0.0)
            out_rows = norm_rows(mixed.reshape(TOK_DEV, ATTN_WIDTH), out_gain.astype(jnp.float32)).astype(jnp.bfloat16)
            return ((new_state, doc_block[-1].astype(jnp.int32)), out_rows)
        start_state = (jnp.zeros((HEADS, HEAD_DIM, HEAD_DIM), jnp.float32), jnp.array(-1, jnp.int32))
        finished, outputs = lax.scan(advance, start_state, (blocks, doc_blocks))
        return outputs.reshape(STREAM, ATTN_WIDTH)
    return lax.map(one_stream, (tokens, doc_ids))
```

```python
import jax
import jax.numpy as jnp
from jax import lax
from jax.sharding import Mesh, PartitionSpec as P

HEADS = 12
HEAD_DIM = 128
ATTN_WIDTH = 1536


EPS = 1e-06


def norm_rows(values, gain):
    mean_sq = jnp.mean(values * values, axis=-1, keepdims=True)
    return values * lax.rsqrt(mean_sq + EPS) * gain


def swap_core(value):
    return lax.ppermute(value, "core", [(0, 1), (1, 0)])


def in_core_order(core, mine, theirs):
    return jnp.where(core == 0, jnp.stack([mine, theirs]), jnp.stack([theirs, mine]))


def mix_block(query_rows, key_rows, value_rows, doc_rows, past_state, past_doc):
    count = doc_rows.shape[1]
    scores = jnp.einsum("sihe,sjhe->shij", query_rows, key_rows, preferred_element_type=jnp.float32)
    row_pos = lax.broadcasted_iota(jnp.int32, (count, count), 0)
    col_pos = lax.broadcasted_iota(jnp.int32, (count, count), 1)
    visible = (row_pos >= col_pos)[None] & (doc_rows[:, :, None] == doc_rows[:, None, :])
    weights = jnp.where(visible[:, None], scores, 0.0).astype(jnp.bfloat16)
    local_part = jnp.einsum(
        "shij,sjhe->sihe", weights, value_rows, preferred_element_type=jnp.float32
    )
    from_past = jnp.einsum(
        "sihe,shef->sihf",
        query_rows,
        past_state.astype(jnp.bfloat16),
        preferred_element_type=jnp.float32,
    )
    joined = (doc_rows == past_doc[:, None])[:, :, None, None]
    return local_part + jnp.where(joined, from_past, 0.0)


def make_shards(n_sq, n_fsdp):
    def shards(tokens, doc_ids, norm_gain, query_weight, key_weight, value_weight, out_gain):
        core = lax.axis_index("core")
        sq = lax.axis_index("sq")
        count, width = tokens.shape[1], tokens.shape[2]
        rows = query_weight.shape[0]
        half = ATTN_WIDTH // 2
        heads = HEADS // 2

        normed = norm_rows(tokens[0].astype(jnp.float32), norm_gain).astype(jnp.bfloat16)
        normed = normed.reshape(count, n_sq, 2, n_fsdp, rows).transpose(0, 1, 3, 2, 4)
        normed = normed.reshape(count, width)
        pair = jnp.concatenate([normed, swap_core(normed)], axis=0)

        def gather_half(weight):
            mine = lax.dynamic_slice_in_dim(weight, core * half, half, axis=1)
            other = lax.dynamic_slice_in_dim(weight, (1 - core) * half, half, axis=1)
            both = in_core_order(core, mine, swap_core(other))
            full = lax.all_gather(both, ("sq", "fsdp"), axis=0, tiled=False)
            return full.reshape(width, half)

        def project(weight):
            summed = jnp.dot(pair, gather_half(weight), preferred_element_type=jnp.float32)
            return jax.nn.silu(summed).astype(jnp.bfloat16).reshape(2, count, heads, HEAD_DIM)

        query_rows = project(query_weight)
        key_rows = project(key_weight)
        value_rows = project(value_weight)

        own_docs = doc_ids[0]
        docs = jnp.stack([own_docs, swap_core(own_docs)])
        first, last = docs[:, 0], docs[:, -1]
        slot_core = jnp.stack([core, 1 - core])
        block = 2 * sq + slot_core

        tail_keys = jnp.where((docs == last[:, None])[:, :, None, None], key_rows, jnp.zeros_like(key_rows))
        tail = jnp.einsum("bjhe,bjhf->bhef", tail_keys, value_rows, preferred_element_type=jnp.float32)
        all_tail = lax.all_gather(tail.astype(jnp.bfloat16), "sq")
        all_last = lax.all_gather(last, "sq")
        all_block = 2 * jnp.arange(n_sq, dtype=jnp.int32)[:, None] + slot_core[None, :]
        counted = (all_block[None] < block[:, None, None]) & (all_last[None] == first[:, None, None])
        carried = jnp.einsum(
            "bsk,skhef->bhef",
            counted.astype(jnp.bfloat16),
            all_tail,
            preferred_element_type=jnp.float32,
        )

        mixed = mix_block(query_rows, key_rows, value_rows, docs, carried, first)
        mixed = mixed.reshape(2, count, half)
        squares = jnp.sum(mixed * mixed, axis=-1)
        total = squares + swap_core(squares)[::-1]
        scale = lax.rsqrt(total / ATTN_WIDTH + EPS)
        gain = lax.dynamic_slice_in_dim(out_gain, core * half, half)
        attended = (mixed * scale[:, :, None] * gain).astype(jnp.bfloat16)
        theirs = swap_core(attended[1])
        out = jnp.where(
            core == 0,
            jnp.concatenate([attended[0], theirs], axis=-1),
            jnp.concatenate([theirs, attended[0]], axis=-1),
        )
        return out[None]

    return shards


def solution(mesh):
    n_seq, n_fsdp = mesh.shape["seq"], mesh.shape["fsdp"]
    chips = Mesh(mesh.devices.reshape(n_seq // 2, 2, n_fsdp), ("sq", "core", "fsdp"))
    seq = ("sq", "core")
    in_specs = (
        P("fsdp", seq, None),
        P("fsdp", seq),
        P(),
        P(("sq", "core", "fsdp"), None),
        P(("sq", "core", "fsdp"), None),
        P(("sq", "core", "fsdp"), None),
        P(),
    )
    out_specs = P("fsdp", seq, None)
    return jax.shard_map(
        make_shards(n_seq // 2, n_fsdp), mesh=chips, in_specs=in_specs, out_specs=out_specs, check_vma=False
    )
```

```python
import jax
import jax.numpy as jnp
from jax import lax
from jax.sharding import Mesh, PartitionSpec as P

HEADS = 12
HEAD_DIM = 128
ATTN_WIDTH = 1536


EPS = 1e-06


def norm_rows(values, gain):
    mean_sq = jnp.mean(values * values, axis=-1, keepdims=True)
    return values * lax.rsqrt(mean_sq + EPS) * gain


def swap_core(value):
    return lax.ppermute(value, "core", [(0, 1), (1, 0)])


def in_core_order(core, mine, theirs):
    return jnp.where(core == 0, jnp.stack([mine, theirs]), jnp.stack([theirs, mine]))


def mix_block(query_rows, key_rows, value_rows, doc_rows, past_state, past_doc):
    count = doc_rows.shape[1]
    scores = jnp.einsum("sihe,sjhe->shij", query_rows, key_rows, preferred_element_type=jnp.float32)
    row_pos = lax.broadcasted_iota(jnp.int32, (count, count), 0)
    col_pos = lax.broadcasted_iota(jnp.int32, (count, count), 1)
    visible = (row_pos >= col_pos)[None] & (doc_rows[:, :, None] == doc_rows[:, None, :])
    weights = jnp.where(visible[:, None], scores, 0.0).astype(jnp.bfloat16)
    local_part = jnp.einsum(
        "shij,sjhe->sihe", weights, value_rows, preferred_element_type=jnp.float32
    )
    from_past = jnp.einsum(
        "sihe,shef->sihf",
        query_rows,
        past_state.astype(jnp.bfloat16),
        preferred_element_type=jnp.float32,
    )
    joined = (doc_rows == past_doc[:, None])[:, :, None, None]
    return local_part + jnp.where(joined, from_past, 0.0)


def make_shards(n_sq, n_fsdp):
    def shards(tokens, doc_ids, norm_gain, query_weight, key_weight, value_weight, out_gain):
        core = lax.axis_index("core")
        sq = lax.axis_index("sq")
        count, width = tokens.shape[1], tokens.shape[2]
        rows = query_weight.shape[0]
        half = ATTN_WIDTH // 2
        heads = HEADS // 2

        normed = norm_rows(tokens[0].astype(jnp.float32), norm_gain).astype(jnp.bfloat16)
        normed = normed.reshape(count, n_sq, 2, n_fsdp, rows).transpose(0, 1, 3, 2, 4)
        normed = normed.reshape(count, width)
        pair = jnp.concatenate([normed, swap_core(normed)], axis=0)

        def halves(start):
            return jnp.concatenate(
                [
                    lax.dynamic_slice_in_dim(weight, start, half, axis=1)
                    for weight in (query_weight, key_weight, value_weight)
                ],
                axis=1,
            )

        mine, other = halves(core * half), halves((1 - core) * half)
        both = in_core_order(core, mine, swap_core(other))
        gathered = lax.all_gather(both, ("sq", "fsdp"), axis=0, tiled=False)
        summed = jnp.dot(pair, gathered.reshape(width, 3 * half), preferred_element_type=jnp.float32)
        query_rows, key_rows, value_rows = [
            jax.nn.silu(summed[:, part * half:(part + 1) * half])
            .astype(jnp.bfloat16)
            .reshape(2, count, heads, HEAD_DIM)
            for part in range(3)
        ]

        own_docs = doc_ids[0]
        docs = jnp.stack([own_docs, swap_core(own_docs)])
        first, last = docs[:, 0], docs[:, -1]
        slot_core = jnp.stack([core, 1 - core])
        block = 2 * sq + slot_core

        tail_keys = jnp.where((docs == last[:, None])[:, :, None, None], key_rows, jnp.zeros_like(key_rows))
        tail = jnp.einsum("bjhe,bjhf->bhef", tail_keys, value_rows, preferred_element_type=jnp.float32)
        all_tail = lax.all_gather(tail.astype(jnp.bfloat16), "sq")
        all_last = lax.all_gather(last, "sq")
        all_block = 2 * jnp.arange(n_sq, dtype=jnp.int32)[:, None] + slot_core[None, :]
        counted = (all_block[None] < block[:, None, None]) & (all_last[None] == first[:, None, None])
        carried = jnp.einsum(
            "bsk,skhef->bhef",
            counted.astype(jnp.bfloat16),
            all_tail,
            preferred_element_type=jnp.float32,
        )

        mixed = mix_block(query_rows, key_rows, value_rows, docs, carried, first)
        mixed = mixed.reshape(2, count, half)
        squares = jnp.sum(mixed * mixed, axis=-1)
        total = squares + swap_core(squares)[::-1]
        scale = lax.rsqrt(total / ATTN_WIDTH + EPS)
        gain = lax.dynamic_slice_in_dim(out_gain, core * half, half)
        attended = (mixed * scale[:, :, None] * gain).astype(jnp.bfloat16)
        theirs = swap_core(attended[1])
        out = jnp.where(
            core == 0,
            jnp.concatenate([attended[0], theirs], axis=-1),
            jnp.concatenate([theirs, attended[0]], axis=-1),
        )
        return out[None]

    return shards


def solution(mesh):
    n_seq, n_fsdp = mesh.shape["seq"], mesh.shape["fsdp"]
    chips = Mesh(mesh.devices.reshape(n_seq // 2, 2, n_fsdp), ("sq", "core", "fsdp"))
    seq = ("sq", "core")
    in_specs = (
        P("fsdp", seq, None),
        P("fsdp", seq),
        P(),
        P(("sq", "core", "fsdp"), None),
        P(("sq", "core", "fsdp"), None),
        P(("sq", "core", "fsdp"), None),
        P(),
    )
    out_specs = P("fsdp", seq, None)
    return jax.shard_map(
        make_shards(n_seq // 2, n_fsdp), mesh=chips, in_specs=in_specs, out_specs=out_specs, check_vma=False
    )
```

```python
import jax
import jax.numpy as jnp
from jax import lax
from jax.sharding import Mesh, PartitionSpec as P

HEADS = 12
HEAD_DIM = 128
ATTN_WIDTH = 1536


EPS = 1e-06


def norm_rows(values, gain):
    mean_sq = jnp.mean(values * values, axis=-1, keepdims=True)
    return values * lax.rsqrt(mean_sq + EPS) * gain


def swap_core(value):
    return lax.ppermute(value, "core", [(0, 1), (1, 0)])


def in_core_order(core, mine, theirs):
    return jnp.where(core == 0, jnp.stack([mine, theirs]), jnp.stack([theirs, mine]))


def mix_block(query_rows, key_rows, value_rows, doc_rows, past_state, past_doc):
    count = doc_rows.shape[1]
    scores = jnp.einsum("sihe,sjhe->shij", query_rows, key_rows, preferred_element_type=jnp.float32)
    row_pos = lax.broadcasted_iota(jnp.int32, (count, count), 0)
    col_pos = lax.broadcasted_iota(jnp.int32, (count, count), 1)
    visible = (row_pos >= col_pos)[None] & (doc_rows[:, :, None] == doc_rows[:, None, :])
    weights = jnp.where(visible[:, None], scores, 0.0).astype(jnp.bfloat16)
    local_part = jnp.einsum(
        "shij,sjhe->sihe", weights, value_rows, preferred_element_type=jnp.float32
    )
    from_past = jnp.einsum(
        "sihe,shef->sihf",
        query_rows,
        past_state.astype(jnp.bfloat16),
        preferred_element_type=jnp.float32,
    )
    joined = (doc_rows == past_doc[:, None])[:, :, None, None]
    return local_part + jnp.where(joined, from_past, 0.0)


def make_shards(n_sq, n_fsdp):
    def shards(tokens, doc_ids, norm_gain, query_weight, key_weight, value_weight, out_gain):
        core = lax.axis_index("core")
        sq = lax.axis_index("sq")
        count, width = tokens.shape[1], tokens.shape[2]
        rows = query_weight.shape[0]
        half = ATTN_WIDTH // 2
        heads = HEADS // 2

        normed = norm_rows(tokens[0].astype(jnp.float32), norm_gain).astype(jnp.bfloat16)
        normed = normed.reshape(count, n_sq, 2, n_fsdp, rows).transpose(0, 1, 3, 2, 4)
        normed = normed.reshape(count, width)
        pair = jnp.concatenate([normed, swap_core(normed)], axis=0)

        def halves(start):
            return jnp.concatenate(
                [
                    lax.dynamic_slice_in_dim(weight, start, half, axis=1)
                    for weight in (query_weight, key_weight, value_weight)
                ],
                axis=1,
            )

        mine, other = halves(core * half), halves((1 - core) * half)
        both = in_core_order(core, mine, swap_core(other))
        gathered = lax.all_gather(both, ("sq", "fsdp"), axis=0, tiled=False)
        summed = jnp.dot(pair, gathered.reshape(width, 3 * half), preferred_element_type=jnp.float32)
        query_rows, key_rows, value_rows = [
            jax.nn.silu(summed[:, part * half:(part + 1) * half])
            .astype(jnp.bfloat16)
            .reshape(2, count, heads, HEAD_DIM)
            for part in range(3)
        ]

        own_docs = doc_ids[0]
        docs = jnp.stack([own_docs, swap_core(own_docs)])
        first, last = docs[:, 0], docs[:, -1]
        slot_core = jnp.stack([core, 1 - core])
        block = 2 * sq + slot_core

        tail_keys = jnp.where((docs == last[:, None])[:, :, None, None], key_rows, jnp.zeros_like(key_rows))
        tail = jnp.einsum("bjhe,bjhf->bhef", tail_keys, value_rows, preferred_element_type=jnp.float32)
        tag = jnp.broadcast_to(last.astype(jnp.bfloat16)[:, None, None], (2, 16, HEAD_DIM))
        message = jnp.concatenate([tail.astype(jnp.bfloat16).reshape(2, heads * HEAD_DIM, HEAD_DIM), tag], axis=1)
        received = [message] + [
            lax.ppermute(message, "sq", [(i, i + shift) for i in range(n_sq - shift)])
            for shift in range(1, n_sq)
        ]
        received = jnp.stack(received)
        all_tail = received[:, :, : heads * HEAD_DIM].reshape(n_sq, 2, heads, HEAD_DIM, HEAD_DIM)
        all_last = received[:, :, heads * HEAD_DIM, 0].astype(jnp.int32)
        shifts = jnp.arange(n_sq, dtype=jnp.int32)[:, None]
        all_block = 2 * (sq - shifts) + slot_core[None, :]
        counted = (
            (shifts <= sq)[None]
            & (all_block[None] < block[:, None, None])
            & (all_last[None] == first[:, None, None])
        )
        carried = jnp.einsum(
            "bsk,skhef->bhef",
            counted.astype(jnp.bfloat16),
            all_tail,
            preferred_element_type=jnp.float32,
        )

        mixed = mix_block(query_rows, key_rows, value_rows, docs, carried, first)
        mixed = mixed.reshape(2, count, half)
        squares = jnp.sum(mixed * mixed, axis=-1)
        total = squares + swap_core(squares)[::-1]
        scale = lax.rsqrt(total / ATTN_WIDTH + EPS)
        gain = lax.dynamic_slice_in_dim(out_gain, core * half, half)
        attended = (mixed * scale[:, :, None] * gain).astype(jnp.bfloat16)
        theirs = swap_core(attended[1])
        out = jnp.where(
            core == 0,
            jnp.concatenate([attended[0], theirs], axis=-1),
            jnp.concatenate([theirs, attended[0]], axis=-1),
        )
        return out[None]

    return shards


def solution(mesh):
    n_seq, n_fsdp = mesh.shape["seq"], mesh.shape["fsdp"]
    chips = Mesh(mesh.devices.reshape(n_seq // 2, 2, n_fsdp), ("sq", "core", "fsdp"))
    seq = ("sq", "core")
    in_specs = (
        P("fsdp", seq, None),
        P("fsdp", seq),
        P(),
        P(("sq", "core", "fsdp"), None),
        P(("sq", "core", "fsdp"), None),
        P(("sq", "core", "fsdp"), None),
        P(),
    )
    out_specs = P("fsdp", seq, None)
    return jax.shard_map(
        make_shards(n_seq // 2, n_fsdp), mesh=chips, in_specs=in_specs, out_specs=out_specs, check_vma=False
    )
```

```python
import jax
import jax.numpy as jnp
from jax import lax
from jax.sharding import Mesh, PartitionSpec as P

HEADS = 12
HEAD_DIM = 128
ATTN_WIDTH = 1536


EPS = 1e-06


def norm_rows(values, gain):
    mean_sq = jnp.mean(values * values, axis=-1, keepdims=True)
    return values * lax.rsqrt(mean_sq + EPS) * gain


def swap_core(value):
    return lax.ppermute(value, "core", [(0, 1), (1, 0)])


def in_core_order(core, mine, theirs):
    return jnp.where(core == 0, jnp.stack([mine, theirs]), jnp.stack([theirs, mine]))


def local_mix(query_rows, key_rows, value_rows, doc_rows):
    count = doc_rows.shape[1]
    scores = jnp.einsum("sihe,sjhe->shij", query_rows, key_rows, preferred_element_type=jnp.float32)
    row_pos = lax.broadcasted_iota(jnp.int32, (count, count), 0)
    col_pos = lax.broadcasted_iota(jnp.int32, (count, count), 1)
    visible = (row_pos >= col_pos)[None] & (doc_rows[:, :, None] == doc_rows[:, None, :])
    weights = jnp.where(visible[:, None], scores, 0.0).astype(jnp.bfloat16)
    return jnp.einsum("shij,sjhe->sihe", weights, value_rows, preferred_element_type=jnp.float32)


def past_mix(local_part, query_rows, doc_rows, past_state, past_doc):
    from_past = jnp.einsum(
        "sihe,shef->sihf",
        query_rows,
        past_state.astype(jnp.bfloat16),
        preferred_element_type=jnp.float32,
    )
    joined = (doc_rows == past_doc[:, None])[:, :, None, None]
    return local_part + jnp.where(joined, from_past, 0.0)


def make_shards(n_sq, n_fsdp):
    def shards(tokens, doc_ids, norm_gain, query_weight, key_weight, value_weight, out_gain):
        core = lax.axis_index("core")
        sq = lax.axis_index("sq")
        count, width = tokens.shape[1], tokens.shape[2]
        rows = query_weight.shape[0]
        half = ATTN_WIDTH // 2
        heads = HEADS // 2

        normed = norm_rows(tokens[0].astype(jnp.float32), norm_gain).astype(jnp.bfloat16)
        normed = normed.reshape(count, n_sq, 2, n_fsdp, rows).transpose(0, 1, 3, 2, 4)
        normed = normed.reshape(count, width)
        pair = jnp.concatenate([normed, swap_core(normed)], axis=0)

        def halves(start):
            return jnp.concatenate(
                [
                    lax.dynamic_slice_in_dim(weight, start, half, axis=1)
                    for weight in (query_weight, key_weight, value_weight)
                ],
                axis=1,
            )

        mine, other = halves(core * half), halves((1 - core) * half)
        both = in_core_order(core, mine, swap_core(other))
        gathered = lax.all_gather(both, ("sq", "fsdp"), axis=0, tiled=False)
        summed = jnp.dot(pair, gathered.reshape(width, 3 * half), preferred_element_type=jnp.float32)
        query_rows, key_rows, value_rows = [
            jax.nn.silu(summed[:, part * half:(part + 1) * half])
            .astype(jnp.bfloat16)
            .reshape(2, count, heads, HEAD_DIM)
            for part in range(3)
        ]

        own_docs = doc_ids[0]
        docs = jnp.stack([own_docs, swap_core(own_docs)])
        first, last = docs[:, 0], docs[:, -1]
        slot_core = jnp.stack([core, 1 - core])
        block = 2 * sq + slot_core

        tail_keys = jnp.where((docs == last[:, None])[:, :, None, None], key_rows, jnp.zeros_like(key_rows))
        tail = jnp.einsum("bjhe,bjhf->bhef", tail_keys, value_rows, preferred_element_type=jnp.float32)
        local_part = lax.optimization_barrier(local_mix(query_rows, key_rows, value_rows, docs))

        tag = jnp.broadcast_to(last.astype(jnp.bfloat16)[:, None, None], (2, 16, HEAD_DIM))
        message = jnp.concatenate([tail.astype(jnp.bfloat16).reshape(2, heads * HEAD_DIM, HEAD_DIM), tag], axis=1)
        received = [message] + [
            lax.ppermute(message, "sq", [(i, i + shift) for i in range(n_sq - shift)])
            for shift in range(1, n_sq)
        ]
        received = jnp.stack(received)
        all_tail = received[:, :, : heads * HEAD_DIM].reshape(n_sq, 2, heads, HEAD_DIM, HEAD_DIM)
        all_last = received[:, :, heads * HEAD_DIM, 0].astype(jnp.int32)
        shifts = jnp.arange(n_sq, dtype=jnp.int32)[:, None]
        all_block = 2 * (sq - shifts) + slot_core[None, :]
        counted = (
            (shifts <= sq)[None]
            & (all_block[None] < block[:, None, None])
            & (all_last[None] == first[:, None, None])
        )
        carried = jnp.einsum(
            "bsk,skhef->bhef",
            counted.astype(jnp.bfloat16),
            all_tail,
            preferred_element_type=jnp.float32,
        )

        mixed = past_mix(local_part, query_rows, docs, carried, first)
        mixed = mixed.reshape(2, count, half)
        squares = jnp.sum(mixed * mixed, axis=-1)
        total = squares + swap_core(squares)[::-1]
        scale = lax.rsqrt(total / ATTN_WIDTH + EPS)
        gain = lax.dynamic_slice_in_dim(out_gain, core * half, half)
        attended = (mixed * scale[:, :, None] * gain).astype(jnp.bfloat16)
        theirs = swap_core(attended[1])
        out = jnp.where(
            core == 0,
            jnp.concatenate([attended[0], theirs], axis=-1),
            jnp.concatenate([theirs, attended[0]], axis=-1),
        )
        return out[None]

    return shards


def solution(mesh):
    n_seq, n_fsdp = mesh.shape["seq"], mesh.shape["fsdp"]
    chips = Mesh(mesh.devices.reshape(n_seq // 2, 2, n_fsdp), ("sq", "core", "fsdp"))
    seq = ("sq", "core")
    in_specs = (
        P("fsdp", seq, None),
        P("fsdp", seq),
        P(),
        P(("sq", "core", "fsdp"), None),
        P(("sq", "core", "fsdp"), None),
        P(("sq", "core", "fsdp"), None),
        P(),
    )
    out_specs = P("fsdp", seq, None)
    return jax.shard_map(
        make_shards(n_seq // 2, n_fsdp), mesh=chips, in_specs=in_specs, out_specs=out_specs, check_vma=False
    )
```

```python
import jax
import jax.numpy as jnp
from jax import lax
from jax.sharding import Mesh, PartitionSpec as P
from jax.experimental import pallas as pl


def _local_kernel(q_ref, k_ref, v_ref, dcol_ref, drow_ref, local_ref):
    q, k = q_ref[...], k_ref[...]
    count = q.shape[0]
    scores = lax.dot_general(q, k, (((1,), (1,)), ((), ())), preferred_element_type=jnp.float32)
    row_pos = lax.broadcasted_iota(jnp.int32, (count, count), 0)
    col_pos = lax.broadcasted_iota(jnp.int32, (count, count), 1)
    visible = (row_pos >= col_pos) & (dcol_ref[...] == drow_ref[...])
    weights = jnp.where(visible, scores, 0.0).astype(jnp.bfloat16)
    local_ref[...] = jnp.dot(weights, v_ref[...], preferred_element_type=jnp.float32)


def _tail_kernel(k_ref, v_ref, dcol_ref, drow_ref, tail_ref):
    k, drow = k_ref[...], drow_ref[...]
    last = drow[:, k.shape[0] - 1:k.shape[0]]
    tail_keys = jnp.where(dcol_ref[...] == last, k, jnp.zeros_like(k))
    tail_ref[...] = lax.dot_general(
        tail_keys, v_ref[...], (((0,), (0,)), ((), ())), preferred_element_type=jnp.float32
    )


def _past_kernel(local_ref, q_ref, state_ref, dcol_ref, drow_ref, out_ref):
    first = drow_ref[...][:, 0:1]
    from_past = jnp.dot(q_ref[...], state_ref[...], preferred_element_type=jnp.float32)
    out_ref[...] = local_ref[...] + jnp.where(dcol_ref[...] == first, from_past, 0.0)


def head_specs(count, heads, parts):
    return [pl.BlockSpec((count, HEAD_DIM), lambda b, h, p=p: (b, p * heads + h)) for p in parts]


def doc_specs(count):
    return [
        pl.BlockSpec((None, count, 1), lambda b, h: (b, 0, 0)),
        pl.BlockSpec((None, 1, count), lambda b, h: (b, 0, 0)),
    ]


def state_spec():
    return pl.BlockSpec((None, None, HEAD_DIM, HEAD_DIM), lambda b, h: (b, h, 0, 0))


def local_attention(qkv, docs, heads):
    blocks, count = docs.shape
    return pl.pallas_call(
        _local_kernel,
        grid=(blocks, heads),
        in_specs=head_specs(count, heads, (0, 1, 2)) + doc_specs(count),
        out_specs=head_specs(count, heads, (0,))[0],
        out_shape=jax.ShapeDtypeStruct((blocks * count, heads * HEAD_DIM), jnp.float32),
    )(qkv, qkv, qkv, docs.reshape(blocks, count, 1), docs.reshape(blocks, 1, count))


def tail_states(qkv, docs, heads):
    blocks, count = docs.shape
    return pl.pallas_call(
        _tail_kernel,
        grid=(blocks, heads),
        in_specs=head_specs(count, heads, (1, 2)) + doc_specs(count),
        out_specs=state_spec(),
        out_shape=jax.ShapeDtypeStruct((blocks, heads, HEAD_DIM, HEAD_DIM), jnp.float32),
    )(qkv, qkv, docs.reshape(blocks, count, 1), docs.reshape(blocks, 1, count))


def add_past(local, qkv, state, docs, heads):
    blocks, count = docs.shape
    tile = head_specs(count, heads, (0,))[0]
    return pl.pallas_call(
        _past_kernel,
        grid=(blocks, heads),
        in_specs=[tile, tile, state_spec()] + doc_specs(count),
        out_specs=tile,
        out_shape=jax.ShapeDtypeStruct(local.shape, jnp.float32),
        input_output_aliases={0: 0},
    )(local, qkv, state, docs.reshape(blocks, count, 1), docs.reshape(blocks, 1, count))

HEADS = 12
HEAD_DIM = 128
ATTN_WIDTH = 1536


EPS = 1e-06


def norm_rows(values, gain):
    mean_sq = jnp.mean(values * values, axis=-1, keepdims=True)
    return values * lax.rsqrt(mean_sq + EPS) * gain


def swap_core(value):
    return lax.ppermute(value, "core", [(0, 1), (1, 0)])


def in_core_order(core, mine, theirs):
    return jnp.where(core == 0, jnp.stack([mine, theirs]), jnp.stack([theirs, mine]))


def make_shards(n_sq, n_fsdp):
    def shards(tokens, doc_ids, norm_gain, query_weight, key_weight, value_weight, out_gain):
        core = lax.axis_index("core")
        sq = lax.axis_index("sq")
        count, width = tokens.shape[1], tokens.shape[2]
        rows = query_weight.shape[0]
        half = ATTN_WIDTH // 2
        heads = HEADS // 2

        normed = norm_rows(tokens[0].astype(jnp.float32), norm_gain).astype(jnp.bfloat16)
        normed = normed.reshape(count, n_sq, 2, n_fsdp, rows).transpose(0, 1, 3, 2, 4)
        normed = normed.reshape(count, width)
        pair = jnp.concatenate([normed, swap_core(normed)], axis=0)

        def halves(start):
            return jnp.concatenate(
                [
                    lax.dynamic_slice_in_dim(weight, start, half, axis=1)
                    for weight in (query_weight, key_weight, value_weight)
                ],
                axis=1,
            )

        mine, other = halves(core * half), halves((1 - core) * half)
        both = in_core_order(core, mine, swap_core(other))
        gathered = lax.all_gather(both, ("sq", "fsdp"), axis=0, tiled=False)
        summed = jnp.dot(pair, gathered.reshape(width, 3 * half), preferred_element_type=jnp.float32)
        qkv = jax.nn.silu(summed).astype(jnp.bfloat16)

        own_docs = doc_ids[0]
        docs = jnp.stack([own_docs, swap_core(own_docs)])
        first, last = docs[:, 0], docs[:, -1]
        slot_core = jnp.stack([core, 1 - core])
        block = 2 * sq + slot_core

        tail = tail_states(qkv, docs, heads)
        local_part = local_attention(qkv, docs, heads)

        tag = jnp.broadcast_to(last.astype(jnp.bfloat16)[:, None, None], (2, 16, HEAD_DIM))
        message = jnp.concatenate([tail.astype(jnp.bfloat16).reshape(2, heads * HEAD_DIM, HEAD_DIM), tag], axis=1)
        received = [message] + [
            lax.ppermute(message, "sq", [(i, i + shift) for i in range(n_sq - shift)])
            for shift in range(1, n_sq)
        ]
        received = jnp.stack(received)
        all_tail = received[:, :, : heads * HEAD_DIM].reshape(n_sq, 2, heads, HEAD_DIM, HEAD_DIM)
        all_last = received[:, :, heads * HEAD_DIM, 0].astype(jnp.int32)
        shifts = jnp.arange(n_sq, dtype=jnp.int32)[:, None]
        all_block = 2 * (sq - shifts) + slot_core[None, :]
        counted = (
            (shifts <= sq)[None]
            & (all_block[None] < block[:, None, None])
            & (all_last[None] == first[:, None, None])
        )
        carried = jnp.einsum(
            "bsk,skhef->bhef",
            counted.astype(jnp.bfloat16),
            all_tail,
            preferred_element_type=jnp.float32,
        )

        mixed = add_past(local_part, qkv, carried.astype(jnp.bfloat16), docs, heads)
        mixed = mixed.reshape(2, count, half)
        squares = jnp.sum(mixed * mixed, axis=-1)
        total = squares + swap_core(squares)[::-1]
        scale = lax.rsqrt(total / ATTN_WIDTH + EPS)
        gain = lax.dynamic_slice_in_dim(out_gain, core * half, half)
        attended = (mixed * scale[:, :, None] * gain).astype(jnp.bfloat16)
        theirs = swap_core(attended[1])
        out = jnp.where(
            core == 0,
            jnp.concatenate([attended[0], theirs], axis=-1),
            jnp.concatenate([theirs, attended[0]], axis=-1),
        )
        return out[None]

    return shards


def solution(mesh):
    n_seq, n_fsdp = mesh.shape["seq"], mesh.shape["fsdp"]
    chips = Mesh(mesh.devices.reshape(n_seq // 2, 2, n_fsdp), ("sq", "core", "fsdp"))
    seq = ("sq", "core")
    in_specs = (
        P("fsdp", seq, None),
        P("fsdp", seq),
        P(),
        P(("sq", "core", "fsdp"), None),
        P(("sq", "core", "fsdp"), None),
        P(("sq", "core", "fsdp"), None),
        P(),
    )
    out_specs = P("fsdp", seq, None)
    return jax.shard_map(
        make_shards(n_seq // 2, n_fsdp), mesh=chips, in_specs=in_specs, out_specs=out_specs, check_vma=False
    )
```

```python
import jax
import jax.numpy as jnp
from jax import lax
from jax.sharding import Mesh, PartitionSpec as P
from jax.experimental import pallas as pl

HEADS = 12
HEAD_DIM = 128
ATTN_WIDTH = 1536


EPS = 1e-06


def norm_rows(values, gain):
    mean_sq = jnp.mean(values * values, axis=-1, keepdims=True)
    return values * lax.rsqrt(mean_sq + EPS) * gain


def swap_core(value):
    return lax.ppermute(value, "core", [(0, 1), (1, 0)])


def in_core_order(core, mine, theirs):
    return jnp.where(core == 0, jnp.stack([mine, theirs]), jnp.stack([theirs, mine]))


def head_columns(ref):
    return [slice(h * HEAD_DIM, (h + 1) * HEAD_DIM) for h in range(ref.shape[1] // HEAD_DIM)]


def _local_kernel(q_ref, k_ref, v_ref, dcol_ref, drow_ref, local_ref):
    count = q_ref.shape[0]
    row_pos = lax.broadcasted_iota(jnp.int32, (count, count), 0)
    col_pos = lax.broadcasted_iota(jnp.int32, (count, count), 1)
    visible = (row_pos >= col_pos) & (dcol_ref[...] == drow_ref[...])
    for cols in head_columns(q_ref):
        scores = lax.dot_general(
            q_ref[:, cols], k_ref[:, cols], (((1,), (1,)), ((), ())), preferred_element_type=jnp.float32
        )
        weights = jnp.where(visible, scores, 0.0).astype(jnp.bfloat16)
        local_ref[:, cols] = jnp.dot(weights, v_ref[:, cols], preferred_element_type=jnp.float32)


def _tail_kernel(k_ref, v_ref, dcol_ref, drow_ref, tail_ref):
    count = k_ref.shape[0]
    ending = dcol_ref[...] == drow_ref[...][:, count - 1:count]
    for h, cols in enumerate(head_columns(k_ref)):
        tail_keys = jnp.where(ending, k_ref[:, cols], jnp.zeros((count, HEAD_DIM), k_ref.dtype))
        tail_ref[h] = lax.dot_general(
            tail_keys, v_ref[:, cols], (((0,), (0,)), ((), ())), preferred_element_type=jnp.float32
        )


def _past_kernel(local_ref, q_ref, state_ref, dcol_ref, drow_ref, out_ref):
    joined = dcol_ref[...] == drow_ref[...][:, 0:1]
    for h, cols in enumerate(head_columns(q_ref)):
        from_past = jnp.dot(q_ref[:, cols], state_ref[h], preferred_element_type=jnp.float32)
        out_ref[:, cols] = local_ref[:, cols] + jnp.where(joined, from_past, 0.0)


def head_specs(count, heads, parts):
    return [pl.BlockSpec((count, heads * HEAD_DIM), lambda b, p=p: (b, p)) for p in parts]


def doc_specs(count):
    return [
        pl.BlockSpec((None, count, 1), lambda b: (b, 0, 0)),
        pl.BlockSpec((None, 1, count), lambda b: (b, 0, 0)),
    ]


def state_spec(heads):
    return pl.BlockSpec((None, heads, HEAD_DIM, HEAD_DIM), lambda b: (b, 0, 0, 0))


def local_attention(qkv, docs, heads):
    blocks, count = docs.shape
    return pl.pallas_call(
        _local_kernel,
        grid=(blocks,),
        in_specs=head_specs(count, heads, (0, 1, 2)) + doc_specs(count),
        out_specs=head_specs(count, heads, (0,))[0],
        out_shape=jax.ShapeDtypeStruct((blocks * count, heads * HEAD_DIM), jnp.float32),
    )(qkv, qkv, qkv, docs.reshape(blocks, count, 1), docs.reshape(blocks, 1, count))


def tail_states(qkv, docs, heads):
    blocks, count = docs.shape
    return pl.pallas_call(
        _tail_kernel,
        grid=(blocks,),
        in_specs=head_specs(count, heads, (1, 2)) + doc_specs(count),
        out_specs=state_spec(heads),
        out_shape=jax.ShapeDtypeStruct((blocks, heads, HEAD_DIM, HEAD_DIM), jnp.float32),
    )(qkv, qkv, docs.reshape(blocks, count, 1), docs.reshape(blocks, 1, count))


def add_past(local, qkv, state, docs, heads):
    blocks, count = docs.shape
    tile = head_specs(count, heads, (0,))[0]
    return pl.pallas_call(
        _past_kernel,
        grid=(blocks,),
        in_specs=[tile, tile, state_spec(heads)] + doc_specs(count),
        out_specs=tile,
        out_shape=jax.ShapeDtypeStruct(local.shape, jnp.float32),
        input_output_aliases={0: 0},
    )(local, qkv, state, docs.reshape(blocks, count, 1), docs.reshape(blocks, 1, count))


def make_shards(n_sq, n_fsdp):
    def shards(tokens, doc_ids, norm_gain, query_weight, key_weight, value_weight, out_gain):
        core = lax.axis_index("core")
        sq = lax.axis_index("sq")
        count, width = tokens.shape[1], tokens.shape[2]
        rows = query_weight.shape[0]
        half = ATTN_WIDTH // 2
        heads = HEADS // 2

        normed = norm_rows(tokens[0].astype(jnp.float32), norm_gain).astype(jnp.bfloat16)
        normed = normed.reshape(count, n_sq, 2, n_fsdp, rows).transpose(0, 1, 3, 2, 4)
        normed = normed.reshape(count, width)
        pair = jnp.concatenate([normed, swap_core(normed)], axis=0)

        def halves(start):
            return jnp.concatenate(
                [
                    lax.dynamic_slice_in_dim(weight, start, half, axis=1)
                    for weight in (query_weight, key_weight, value_weight)
                ],
                axis=1,
            )

        mine, other = halves(core * half), halves((1 - core) * half)
        both = in_core_order(core, mine, swap_core(other))
        gathered = lax.all_gather(both, ("sq", "fsdp"), axis=0, tiled=False)
        summed = jnp.dot(pair, gathered.reshape(width, 3 * half), preferred_element_type=jnp.float32)
        qkv = jax.nn.silu(summed).astype(jnp.bfloat16)

        own_docs = doc_ids[0]
        docs = jnp.stack([own_docs, swap_core(own_docs)])
        first, last = docs[:, 0], docs[:, -1]
        slot_core = jnp.stack([core, 1 - core])
        block = 2 * sq + slot_core

        tail = tail_states(qkv, docs, heads)
        local_part = local_attention(qkv, docs, heads)

        tag = jnp.broadcast_to(last.astype(jnp.bfloat16)[:, None, None], (2, 16, HEAD_DIM))
        message = jnp.concatenate([tail.astype(jnp.bfloat16).reshape(2, heads * HEAD_DIM, HEAD_DIM), tag], axis=1)
        received = [message] + [
            lax.ppermute(message, "sq", [(i, i + shift) for i in range(n_sq - shift)])
            for shift in range(1, n_sq)
        ]
        received = jnp.stack(received)
        all_tail = received[:, :, : heads * HEAD_DIM].reshape(n_sq, 2, heads, HEAD_DIM, HEAD_DIM)
        all_last = received[:, :, heads * HEAD_DIM, 0].astype(jnp.int32)
        shifts = jnp.arange(n_sq, dtype=jnp.int32)[:, None]
        all_block = 2 * (sq - shifts) + slot_core[None, :]
        counted = (
            (shifts <= sq)[None]
            & (all_block[None] < block[:, None, None])
            & (all_last[None] == first[:, None, None])
        )
        carried = jnp.einsum(
            "bsk,skhef->bhef",
            counted.astype(jnp.bfloat16),
            all_tail,
            preferred_element_type=jnp.float32,
        )

        mixed = add_past(local_part, qkv, carried.astype(jnp.bfloat16), docs, heads)
        mixed = mixed.reshape(2, count, half)
        squares = jnp.sum(mixed * mixed, axis=-1)
        total = squares + swap_core(squares)[::-1]
        scale = lax.rsqrt(total / ATTN_WIDTH + EPS)
        gain = lax.dynamic_slice_in_dim(out_gain, core * half, half)
        attended = (mixed * scale[:, :, None] * gain).astype(jnp.bfloat16)
        theirs = swap_core(attended[1])
        out = jnp.where(
            core == 0,
            jnp.concatenate([attended[0], theirs], axis=-1),
            jnp.concatenate([theirs, attended[0]], axis=-1),
        )
        return out[None]

    return shards


def solution(mesh):
    n_seq, n_fsdp = mesh.shape["seq"], mesh.shape["fsdp"]
    chips = Mesh(mesh.devices.reshape(n_seq // 2, 2, n_fsdp), ("sq", "core", "fsdp"))
    seq = ("sq", "core")
    in_specs = (
        P("fsdp", seq, None),
        P("fsdp", seq),
        P(),
        P(("sq", "core", "fsdp"), None),
        P(("sq", "core", "fsdp"), None),
        P(("sq", "core", "fsdp"), None),
        P(),
    )
    out_specs = P("fsdp", seq, None)
    return jax.shard_map(
        make_shards(n_seq // 2, n_fsdp), mesh=chips, in_specs=in_specs, out_specs=out_specs, check_vma=False
    )
```

```python
import jax
import jax.numpy as jnp
from jax import lax
from jax.sharding import Mesh, PartitionSpec as P
from jax.experimental import pallas as pl

HEADS = 12
HEAD_DIM = 128
ATTN_WIDTH = 1536


EPS = 1e-06


def norm_rows(values, gain):
    mean_sq = jnp.mean(values * values, axis=-1, keepdims=True)
    return values * lax.rsqrt(mean_sq + EPS) * gain


def swap_core(value):
    return lax.ppermute(value, "core", [(0, 1), (1, 0)])


def in_core_order(core, mine, theirs):
    return jnp.where(core == 0, jnp.stack([mine, theirs]), jnp.stack([theirs, mine]))


def head_columns(ref):
    return [slice(h * HEAD_DIM, (h + 1) * HEAD_DIM) for h in range(ref.shape[1] // HEAD_DIM)]


def _local_kernel(q_ref, k_ref, v_ref, dcol_ref, drow_ref, local_ref):
    count = q_ref.shape[0]
    row_pos = lax.broadcasted_iota(jnp.int32, (count, count), 0)
    col_pos = lax.broadcasted_iota(jnp.int32, (count, count), 1)
    visible = (row_pos >= col_pos) & (dcol_ref[...] == drow_ref[...])
    for cols in head_columns(q_ref):
        scores = lax.dot_general(
            q_ref[:, cols], k_ref[:, cols], (((1,), (1,)), ((), ())), preferred_element_type=jnp.float32
        )
        weights = jnp.where(visible, scores, 0.0).astype(jnp.bfloat16)
        local_ref[:, cols] = jnp.dot(weights, v_ref[:, cols], preferred_element_type=jnp.float32)


def _tail_kernel(k_ref, v_ref, dcol_ref, drow_ref, tail_ref):
    count = k_ref.shape[0]
    ending = dcol_ref[...] == drow_ref[...][:, count - 1:count]
    for h, cols in enumerate(head_columns(k_ref)):
        tail_keys = jnp.where(ending, k_ref[:, cols], jnp.zeros((count, HEAD_DIM), k_ref.dtype))
        tail_ref[h] = lax.dot_general(
            tail_keys, v_ref[:, cols], (((0,), (0,)), ((), ())), preferred_element_type=jnp.float32
        )


def _past_kernel(local_ref, q_ref, state_ref, dcol_ref, drow_ref, out_ref):
    joined = dcol_ref[...] == drow_ref[...][:, 0:1]
    for h, cols in enumerate(head_columns(q_ref)):
        from_past = jnp.dot(q_ref[:, cols], state_ref[h], preferred_element_type=jnp.float32)
        out_ref[:, cols] = local_ref[:, cols] + jnp.where(joined, from_past, 0.0)


def head_specs(count, heads, parts):
    return [pl.BlockSpec((count, heads * HEAD_DIM), lambda b, p=p: (b, p)) for p in parts]


def doc_specs(count):
    return [
        pl.BlockSpec((None, count, 1), lambda b: (b, 0, 0)),
        pl.BlockSpec((None, 1, count), lambda b: (b, 0, 0)),
    ]


def state_spec(heads):
    return pl.BlockSpec((None, heads, HEAD_DIM, HEAD_DIM), lambda b: (b, 0, 0, 0))


def local_attention(query, key_value, docs, heads):
    blocks, count = docs.shape
    return pl.pallas_call(
        _local_kernel,
        grid=(blocks,),
        in_specs=head_specs(count, heads, (0, 0, 1)) + doc_specs(count),
        out_specs=head_specs(count, heads, (0,))[0],
        out_shape=jax.ShapeDtypeStruct((blocks * count, heads * HEAD_DIM), jnp.float32),
    )(query, key_value, key_value, docs.reshape(blocks, count, 1), docs.reshape(blocks, 1, count))


def tail_states(key_value, docs, heads):
    blocks, count = docs.shape
    return pl.pallas_call(
        _tail_kernel,
        grid=(blocks,),
        in_specs=head_specs(count, heads, (0, 1)) + doc_specs(count),
        out_specs=state_spec(heads),
        out_shape=jax.ShapeDtypeStruct((blocks, heads, HEAD_DIM, HEAD_DIM), jnp.float32),
    )(key_value, key_value, docs.reshape(blocks, count, 1), docs.reshape(blocks, 1, count))


def add_past(local, query, state, docs, heads):
    blocks, count = docs.shape
    tile = head_specs(count, heads, (0,))[0]
    return pl.pallas_call(
        _past_kernel,
        grid=(blocks,),
        in_specs=[tile, tile, state_spec(heads)] + doc_specs(count),
        out_specs=tile,
        out_shape=jax.ShapeDtypeStruct(local.shape, jnp.float32),
        input_output_aliases={0: 0},
    )(local, query, state, docs.reshape(blocks, count, 1), docs.reshape(blocks, 1, count))


def make_shards(n_sq, n_fsdp):
    def shards(tokens, doc_ids, norm_gain, query_weight, key_weight, value_weight, out_gain):
        core = lax.axis_index("core")
        sq = lax.axis_index("sq")
        count, width = tokens.shape[1], tokens.shape[2]
        rows = query_weight.shape[0]
        half = ATTN_WIDTH // 2
        heads = HEADS // 2

        normed = norm_rows(tokens[0].astype(jnp.float32), norm_gain).astype(jnp.bfloat16)
        normed = normed.reshape(count, n_sq, 2, n_fsdp, rows).transpose(0, 1, 3, 2, 4)
        normed = normed.reshape(count, width)
        pair = jnp.concatenate([normed, swap_core(normed)], axis=0)

        def halves(start):
            return jnp.concatenate(
                [
                    lax.dynamic_slice_in_dim(weight, start, half, axis=1)
                    for weight in (query_weight, key_weight, value_weight)
                ],
                axis=1,
            )

        mine, other = halves(core * half), halves((1 - core) * half)
        both = in_core_order(core, mine, swap_core(other))
        gathered = lax.all_gather(both, ("sq", "fsdp"), axis=0, tiled=False)
        weights = gathered.reshape(width, 3 * half)

        def project(columns):
            summed = jnp.dot(pair, columns, preferred_element_type=jnp.float32)
            return jax.nn.silu(summed).astype(jnp.bfloat16)

        key_value = project(weights[:, half:])

        own_docs = doc_ids[0]
        docs = jnp.stack([own_docs, swap_core(own_docs)])
        first, last = docs[:, 0], docs[:, -1]
        slot_core = jnp.stack([core, 1 - core])
        block = 2 * sq + slot_core

        tail = tail_states(key_value, docs, heads)
        query = project(weights[:, :half])
        local_part = local_attention(query, key_value, docs, heads)

        tag = jnp.broadcast_to(last.astype(jnp.bfloat16)[:, None, None], (2, 16, HEAD_DIM))
        message = jnp.concatenate([tail.astype(jnp.bfloat16).reshape(2, heads * HEAD_DIM, HEAD_DIM), tag], axis=1)
        received = [message] + [
            lax.ppermute(message, "sq", [(i, i + shift) for i in range(n_sq - shift)])
            for shift in range(1, n_sq)
        ]
        received = jnp.stack(received)
        all_tail = received[:, :, : heads * HEAD_DIM].reshape(n_sq, 2, heads, HEAD_DIM, HEAD_DIM)
        all_last = received[:, :, heads * HEAD_DIM, 0].astype(jnp.int32)
        shifts = jnp.arange(n_sq, dtype=jnp.int32)[:, None]
        all_block = 2 * (sq - shifts) + slot_core[None, :]
        counted = (
            (shifts <= sq)[None]
            & (all_block[None] < block[:, None, None])
            & (all_last[None] == first[:, None, None])
        )
        carried = jnp.einsum(
            "bsk,skhef->bhef",
            counted.astype(jnp.bfloat16),
            all_tail,
            preferred_element_type=jnp.float32,
        )

        mixed = add_past(local_part, query, carried.astype(jnp.bfloat16), docs, heads)
        mixed = mixed.reshape(2, count, half)
        squares = jnp.sum(mixed * mixed, axis=-1)
        total = squares + swap_core(squares)[::-1]
        scale = lax.rsqrt(total / ATTN_WIDTH + EPS)
        gain = lax.dynamic_slice_in_dim(out_gain, core * half, half)
        attended = (mixed * scale[:, :, None] * gain).astype(jnp.bfloat16)
        theirs = swap_core(attended[1])
        out = jnp.where(
            core == 0,
            jnp.concatenate([attended[0], theirs], axis=-1),
            jnp.concatenate([theirs, attended[0]], axis=-1),
        )
        return out[None]

    return shards


def solution(mesh):
    n_seq, n_fsdp = mesh.shape["seq"], mesh.shape["fsdp"]
    chips = Mesh(mesh.devices.reshape(n_seq // 2, 2, n_fsdp), ("sq", "core", "fsdp"))
    seq = ("sq", "core")
    in_specs = (
        P("fsdp", seq, None),
        P("fsdp", seq),
        P(),
        P(("sq", "core", "fsdp"), None),
        P(("sq", "core", "fsdp"), None),
        P(("sq", "core", "fsdp"), None),
        P(),
    )
    out_specs = P("fsdp", seq, None)
    return jax.shard_map(
        make_shards(n_seq // 2, n_fsdp), mesh=chips, in_specs=in_specs, out_specs=out_specs, check_vma=False
    )
```

```python
import jax
import jax.numpy as jnp
from jax import lax
from jax.sharding import Mesh, PartitionSpec as P
from jax.experimental import pallas as pl

HEADS = 12
HEAD_DIM = 128
ATTN_WIDTH = 1536


EPS = 1e-06


def norm_rows(values, gain):
    mean_sq = jnp.mean(values * values, axis=-1, keepdims=True)
    return values * lax.rsqrt(mean_sq + EPS) * gain


def swap_core(value):
    return lax.ppermute(value, "core", [(0, 1), (1, 0)])


def in_core_order(core, mine, theirs):
    return jnp.where(core == 0, jnp.stack([mine, theirs]), jnp.stack([theirs, mine]))


def head_columns(ref):
    return [slice(h * HEAD_DIM, (h + 1) * HEAD_DIM) for h in range(ref.shape[1] // HEAD_DIM)]


def _local_kernel(q_ref, k_ref, v_ref, dcol_ref, drow_ref, local_ref):
    count = q_ref.shape[0]
    row_pos = lax.broadcasted_iota(jnp.int32, (count, count), 0)
    col_pos = lax.broadcasted_iota(jnp.int32, (count, count), 1)
    visible = (row_pos >= col_pos) & (dcol_ref[...] == drow_ref[...])
    for cols in head_columns(q_ref):
        scores = lax.dot_general(
            q_ref[:, cols], k_ref[:, cols], (((1,), (1,)), ((), ())), preferred_element_type=jnp.float32
        )
        weights = jnp.where(visible, scores, 0.0).astype(jnp.bfloat16)
        local_ref[:, cols] = jnp.dot(weights, v_ref[:, cols], preferred_element_type=jnp.float32)


def _tail_kernel(k_ref, v_ref, dcol_ref, drow_ref, tail_ref):
    count = k_ref.shape[0]
    ending = dcol_ref[...] == drow_ref[...][:, count - 1:count]
    for h, cols in enumerate(head_columns(k_ref)):
        tail_keys = jnp.where(ending, k_ref[:, cols], jnp.zeros((count, HEAD_DIM), k_ref.dtype))
        tail_ref[h] = lax.dot_general(
            tail_keys, v_ref[:, cols], (((0,), (0,)), ((), ())), preferred_element_type=jnp.float32
        )


def _past_kernel(local_ref, q_ref, state_ref, dcol_ref, drow_ref, out_ref, squares_ref):
    joined = dcol_ref[...] == drow_ref[...][:, 0:1]
    squares = jnp.zeros((q_ref.shape[0], 1), jnp.float32)
    for h, cols in enumerate(head_columns(q_ref)):
        from_past = jnp.dot(q_ref[:, cols], state_ref[h], preferred_element_type=jnp.float32)
        mixed = local_ref[:, cols] + jnp.where(joined, from_past, 0.0)
        out_ref[:, cols] = mixed
        squares = squares + jnp.sum(mixed * mixed, axis=1, keepdims=True)
    squares_ref[...] = squares


def head_specs(count, heads, parts):
    return [pl.BlockSpec((count, heads * HEAD_DIM), lambda b, p=p: (b, p)) for p in parts]


def doc_specs(count):
    return [
        pl.BlockSpec((None, count, 1), lambda b: (b, 0, 0)),
        pl.BlockSpec((None, 1, count), lambda b: (b, 0, 0)),
    ]


def state_spec(heads):
    return pl.BlockSpec((None, heads, HEAD_DIM, HEAD_DIM), lambda b: (b, 0, 0, 0))


def local_attention(qkv, docs, heads):
    blocks, count = docs.shape
    return pl.pallas_call(
        _local_kernel,
        grid=(blocks,),
        in_specs=head_specs(count, heads, (0, 1, 2)) + doc_specs(count),
        out_specs=head_specs(count, heads, (0,))[0],
        out_shape=jax.ShapeDtypeStruct((blocks * count, heads * HEAD_DIM), jnp.float32),
    )(qkv, qkv, qkv, docs.reshape(blocks, count, 1), docs.reshape(blocks, 1, count))


def tail_states(qkv, docs, heads):
    blocks, count = docs.shape
    return pl.pallas_call(
        _tail_kernel,
        grid=(blocks,),
        in_specs=head_specs(count, heads, (1, 2)) + doc_specs(count),
        out_specs=state_spec(heads),
        out_shape=jax.ShapeDtypeStruct((blocks, heads, HEAD_DIM, HEAD_DIM), jnp.float32),
    )(qkv, qkv, docs.reshape(blocks, count, 1), docs.reshape(blocks, 1, count))


def add_past(local, qkv, state, docs, heads):
    blocks, count = docs.shape
    tile = head_specs(count, heads, (0,))[0]
    return pl.pallas_call(
        _past_kernel,
        grid=(blocks,),
        in_specs=[tile, tile, state_spec(heads)] + doc_specs(count),
        out_specs=[tile, pl.BlockSpec((count, 1), lambda b: (b, 0))],
        out_shape=[
            jax.ShapeDtypeStruct(local.shape, jnp.float32),
            jax.ShapeDtypeStruct((blocks * count, 1), jnp.float32),
        ],
        input_output_aliases={0: 0},
    )(local, qkv, state, docs.reshape(blocks, count, 1), docs.reshape(blocks, 1, count))


def make_shards(n_sq, n_fsdp):
    def shards(tokens, doc_ids, norm_gain, query_weight, key_weight, value_weight, out_gain):
        core = lax.axis_index("core")
        sq = lax.axis_index("sq")
        count, width = tokens.shape[1], tokens.shape[2]
        rows = query_weight.shape[0]
        half = ATTN_WIDTH // 2
        heads = HEADS // 2

        normed = norm_rows(tokens[0].astype(jnp.float32), norm_gain).astype(jnp.bfloat16)
        normed = normed.reshape(count, n_sq, 2, n_fsdp, rows).transpose(0, 1, 3, 2, 4)
        normed = normed.reshape(count, width)
        pair = jnp.concatenate([normed, swap_core(normed)], axis=0)

        def halves(start):
            return jnp.concatenate(
                [
                    lax.dynamic_slice_in_dim(weight, start, half, axis=1)
                    for weight in (query_weight, key_weight, value_weight)
                ],
                axis=1,
            )

        mine, other = halves(core * half), halves((1 - core) * half)
        both = in_core_order(core, mine, swap_core(other))
        gathered = lax.all_gather(both, ("sq", "fsdp"), axis=0, tiled=False)
        summed = jnp.dot(pair, gathered.reshape(width, 3 * half), preferred_element_type=jnp.float32)
        qkv = jax.nn.silu(summed).astype(jnp.bfloat16)

        own_docs = doc_ids[0]
        docs = jnp.stack([own_docs, swap_core(own_docs)])
        first, last = docs[:, 0], docs[:, -1]
        slot_core = jnp.stack([core, 1 - core])
        block = 2 * sq + slot_core

        tail = tail_states(qkv, docs, heads)
        local_part = local_attention(qkv, docs, heads)

        tag = jnp.broadcast_to(last.astype(jnp.bfloat16)[:, None, None], (2, 16, HEAD_DIM))
        message = jnp.concatenate([tail.astype(jnp.bfloat16).reshape(2, heads * HEAD_DIM, HEAD_DIM), tag], axis=1)
        received = [message] + [
            lax.ppermute(message, "sq", [(i, i + shift) for i in range(n_sq - shift)])
            for shift in range(1, n_sq)
        ]
        received = jnp.stack(received)
        all_tail = received[:, :, : heads * HEAD_DIM].reshape(n_sq, 2, heads, HEAD_DIM, HEAD_DIM)
        all_last = received[:, :, heads * HEAD_DIM, 0].astype(jnp.int32)
        shifts = jnp.arange(n_sq, dtype=jnp.int32)[:, None]
        all_block = 2 * (sq - shifts) + slot_core[None, :]
        counted = (
            (shifts <= sq)[None]
            & (all_block[None] < block[:, None, None])
            & (all_last[None] == first[:, None, None])
        )
        carried = jnp.einsum(
            "bsk,skhef->bhef",
            counted.astype(jnp.bfloat16),
            all_tail,
            preferred_element_type=jnp.float32,
        )

        mixed, squares = add_past(local_part, qkv, carried.astype(jnp.bfloat16), docs, heads)
        mixed = mixed.reshape(2, count, half)
        squares = squares.reshape(2, count)
        total = squares + swap_core(squares)[::-1]
        scale = lax.rsqrt(total / ATTN_WIDTH + EPS)
        gain = lax.dynamic_slice_in_dim(out_gain, core * half, half)
        attended = (mixed * scale[:, :, None] * gain).astype(jnp.bfloat16)
        theirs = swap_core(attended[1])
        out = jnp.where(
            core == 0,
            jnp.concatenate([attended[0], theirs], axis=-1),
            jnp.concatenate([theirs, attended[0]], axis=-1),
        )
        return out[None]

    return shards


def solution(mesh):
    n_seq, n_fsdp = mesh.shape["seq"], mesh.shape["fsdp"]
    chips = Mesh(mesh.devices.reshape(n_seq // 2, 2, n_fsdp), ("sq", "core", "fsdp"))
    seq = ("sq", "core")
    in_specs = (
        P("fsdp", seq, None),
        P("fsdp", seq),
        P(),
        P(("sq", "core", "fsdp"), None),
        P(("sq", "core", "fsdp"), None),
        P(("sq", "core", "fsdp"), None),
        P(),
    )
    out_specs = P("fsdp", seq, None)
    return jax.shard_map(
        make_shards(n_seq // 2, n_fsdp), mesh=chips, in_specs=in_specs, out_specs=out_specs, check_vma=False
    )
```

```python
import jax
import jax.numpy as jnp
from jax import lax
from jax.sharding import Mesh, PartitionSpec as P
from jax.experimental import pallas as pl

HEADS = 12
HEAD_DIM = 128
ATTN_WIDTH = 1536


EPS = 1e-06


def norm_rows(values, gain):
    mean_sq = jnp.mean(values * values, axis=-1, keepdims=True)
    return values * lax.rsqrt(mean_sq + EPS) * gain


def swap_core(value):
    return lax.ppermute(value, "core", [(0, 1), (1, 0)])


def in_core_order(core, mine, theirs):
    return jnp.where(core == 0, jnp.stack([mine, theirs]), jnp.stack([theirs, mine]))


def head_columns(ref):
    return [slice(h * HEAD_DIM, (h + 1) * HEAD_DIM) for h in range(ref.shape[1] // HEAD_DIM)]


def _local_kernel(q_ref, k_ref, v_ref, dcol_ref, drow_ref, local_ref):
    count = q_ref.shape[0]
    row_pos = lax.broadcasted_iota(jnp.int32, (count, count), 0)
    col_pos = lax.broadcasted_iota(jnp.int32, (count, count), 1)
    visible = (row_pos >= col_pos) & (dcol_ref[...] == drow_ref[...])
    for cols in head_columns(q_ref):
        scores = lax.dot_general(
            q_ref[:, cols], k_ref[:, cols], (((1,), (1,)), ((), ())), preferred_element_type=jnp.float32
        )
        weights = jnp.where(visible, scores, 0.0).astype(jnp.bfloat16)
        local_ref[:, cols] = jnp.dot(weights, v_ref[:, cols], preferred_element_type=jnp.float32)


def _tail_kernel(k_ref, v_ref, dcol_ref, drow_ref, tail_ref):
    count = k_ref.shape[0]
    ending = dcol_ref[...] == drow_ref[...][:, count - 1:count]
    for h, cols in enumerate(head_columns(k_ref)):
        tail_keys = jnp.where(ending, k_ref[:, cols], jnp.zeros((count, HEAD_DIM), k_ref.dtype))
        tail_ref[h] = lax.dot_general(
            tail_keys, v_ref[:, cols], (((0,), (0,)), ((), ())), preferred_element_type=jnp.float32
        )


def _past_kernel(local_ref, q_ref, state_ref, dcol_ref, drow_ref, out_ref):
    joined = dcol_ref[...] == drow_ref[...][:, 0:1]
    for h, cols in enumerate(head_columns(q_ref)):
        from_past = jnp.dot(q_ref[:, cols], state_ref[h], preferred_element_type=jnp.float32)
        out_ref[:, cols] = local_ref[:, cols] + jnp.where(joined, from_past, 0.0)


def head_specs(count, heads, parts):
    return [pl.BlockSpec((count, heads * HEAD_DIM), lambda b, p=p: (b, p)) for p in parts]


def doc_specs(count):
    return [
        pl.BlockSpec((None, count, 1), lambda b: (b, 0, 0)),
        pl.BlockSpec((None, 1, count), lambda b: (b, 0, 0)),
    ]


def state_spec(heads):
    return pl.BlockSpec((None, heads, HEAD_DIM, HEAD_DIM), lambda b: (b, 0, 0, 0))


def local_attention(qkv, docs, heads):
    blocks, count = docs.shape
    return pl.pallas_call(
        _local_kernel,
        grid=(blocks,),
        in_specs=head_specs(count, heads, (0, 1, 2)) + doc_specs(count),
        out_specs=head_specs(count, heads, (0,))[0],
        out_shape=jax.ShapeDtypeStruct((blocks * count, heads * HEAD_DIM), jnp.float32),
    )(qkv, qkv, qkv, docs.reshape(blocks, count, 1), docs.reshape(blocks, 1, count))


def tail_states(qkv, docs, heads):
    blocks, count = docs.shape
    return pl.pallas_call(
        _tail_kernel,
        grid=(blocks,),
        in_specs=head_specs(count, heads, (1, 2)) + doc_specs(count),
        out_specs=state_spec(heads),
        out_shape=jax.ShapeDtypeStruct((blocks, heads, HEAD_DIM, HEAD_DIM), jnp.float32),
    )(qkv, qkv, docs.reshape(blocks, count, 1), docs.reshape(blocks, 1, count))


def add_past(local, qkv, state, docs, heads):
    blocks, count = docs.shape
    tile = head_specs(count, heads, (0,))[0]
    return pl.pallas_call(
        _past_kernel,
        grid=(blocks,),
        in_specs=[tile, tile, state_spec(heads)] + doc_specs(count),
        out_specs=tile,
        out_shape=jax.ShapeDtypeStruct(local.shape, jnp.float32),
        input_output_aliases={0: 0},
    )(local, qkv, state, docs.reshape(blocks, count, 1), docs.reshape(blocks, 1, count))


def make_shards(n_sq, n_fsdp):
    def shards(tokens, doc_ids, norm_gain, query_weight, key_weight, value_weight, out_gain):
        core = lax.axis_index("core")
        sq = lax.axis_index("sq")
        count, width = tokens.shape[1], tokens.shape[2]
        rows = query_weight.shape[0]
        half = ATTN_WIDTH // 2
        heads = HEADS // 2

        def halves(start):
            return jnp.concatenate(
                [
                    lax.dynamic_slice_in_dim(weight, start, half, axis=1)
                    for weight in (query_weight, key_weight, value_weight)
                ],
                axis=1,
            )

        both = jnp.stack([halves(core * half), halves((1 - core) * half)])
        gathered = lax.all_gather(both, ("sq", "fsdp"), axis=0, tiled=False)
        own_rows = gathered[:, 0].reshape(n_sq * n_fsdp * rows, 3 * half)
        sibling_rows = swap_core(gathered[:, 1]).reshape(n_sq * n_fsdp * rows, 3 * half)

        normed = norm_rows(tokens[0].astype(jnp.float32), norm_gain).astype(jnp.bfloat16)
        pair = jnp.concatenate([normed, swap_core(normed)], axis=0).reshape(2 * count, n_sq, 2, n_fsdp, rows)
        by_core = [pair[:, :, slot].reshape(2 * count, n_sq * n_fsdp * rows) for slot in range(2)]
        own_features = jnp.where(core == 0, by_core[0], by_core[1])
        sibling_features = jnp.where(core == 0, by_core[1], by_core[0])
        summed = jnp.dot(own_features, own_rows, preferred_element_type=jnp.float32)
        summed = summed + jnp.dot(sibling_features, sibling_rows, preferred_element_type=jnp.float32)
        qkv = jax.nn.silu(summed).astype(jnp.bfloat16)

        own_docs = doc_ids[0]
        docs = jnp.stack([own_docs, swap_core(own_docs)])
        first, last = docs[:, 0], docs[:, -1]
        slot_core = jnp.stack([core, 1 - core])
        block = 2 * sq + slot_core

        tail = tail_states(qkv, docs, heads)
        local_part = local_attention(qkv, docs, heads)

        tag = jnp.broadcast_to(last.astype(jnp.bfloat16)[:, None, None], (2, 16, HEAD_DIM))
        message = jnp.concatenate([tail.astype(jnp.bfloat16).reshape(2, heads * HEAD_DIM, HEAD_DIM), tag], axis=1)
        received = [message] + [
            lax.ppermute(message, "sq", [(i, i + shift) for i in range(n_sq - shift)])
            for shift in range(1, n_sq)
        ]
        received = jnp.stack(received)
        all_tail = received[:, :, : heads * HEAD_DIM].reshape(n_sq, 2, heads, HEAD_DIM, HEAD_DIM)
        all_last = received[:, :, heads * HEAD_DIM, 0].astype(jnp.int32)
        shifts = jnp.arange(n_sq, dtype=jnp.int32)[:, None]
        all_block = 2 * (sq - shifts) + slot_core[None, :]
        counted = (
            (shifts <= sq)[None]
            & (all_block[None] < block[:, None, None])
            & (all_last[None] == first[:, None, None])
        )
        carried = jnp.einsum(
            "bsk,skhef->bhef",
            counted.astype(jnp.bfloat16),
            all_tail,
            preferred_element_type=jnp.float32,
        )

        mixed = add_past(local_part, qkv, carried.astype(jnp.bfloat16), docs, heads)
        mixed = mixed.reshape(2, count, half)
        squares = jnp.sum(mixed * mixed, axis=-1)
        total = squares + swap_core(squares)[::-1]
        scale = lax.rsqrt(total / ATTN_WIDTH + EPS)
        gain = lax.dynamic_slice_in_dim(out_gain, core * half, half)
        attended = (mixed * scale[:, :, None] * gain).astype(jnp.bfloat16)
        theirs = swap_core(attended[1])
        out = jnp.where(
            core == 0,
            jnp.concatenate([attended[0], theirs], axis=-1),
            jnp.concatenate([theirs, attended[0]], axis=-1),
        )
        return out[None]

    return shards


def solution(mesh):
    n_seq, n_fsdp = mesh.shape["seq"], mesh.shape["fsdp"]
    chips = Mesh(mesh.devices.reshape(n_seq // 2, 2, n_fsdp), ("sq", "core", "fsdp"))
    seq = ("sq", "core")
    in_specs = (
        P("fsdp", seq, None),
        P("fsdp", seq),
        P(),
        P(("sq", "core", "fsdp"), None),
        P(("sq", "core", "fsdp"), None),
        P(("sq", "core", "fsdp"), None),
        P(),
    )
    out_specs = P("fsdp", seq, None)
    return jax.shard_map(
        make_shards(n_seq // 2, n_fsdp), mesh=chips, in_specs=in_specs, out_specs=out_specs, check_vma=False
    )
```

```python
import jax
import jax.numpy as jnp
from jax import lax
from jax.sharding import Mesh, PartitionSpec as P
from jax.experimental import pallas as pl

HEADS = 12
HEAD_DIM = 128
ATTN_WIDTH = 1536


EPS = 1e-06


def norm_rows(values, gain):
    mean_sq = jnp.mean(values * values, axis=-1, keepdims=True)
    return values * lax.rsqrt(mean_sq + EPS) * gain


def swap_core(value):
    return lax.ppermute(value, "core", [(0, 1), (1, 0)])


def in_core_order(core, mine, theirs):
    return jnp.where(core == 0, jnp.stack([mine, theirs]), jnp.stack([theirs, mine]))


def head_columns(ref):
    return [slice(h * HEAD_DIM, (h + 1) * HEAD_DIM) for h in range(ref.shape[1] // HEAD_DIM)]


def _local_kernel(q_ref, k_ref, v_ref, dcol_ref, drow_ref, local_ref):
    count = q_ref.shape[0]
    row_pos = lax.broadcasted_iota(jnp.int32, (count, count), 0)
    col_pos = lax.broadcasted_iota(jnp.int32, (count, count), 1)
    visible = (row_pos >= col_pos) & (dcol_ref[...] == drow_ref[...])
    for cols in head_columns(q_ref):
        scores = lax.dot_general(
            q_ref[:, cols], k_ref[:, cols], (((1,), (1,)), ((), ())), preferred_element_type=jnp.float32
        )
        weights = jnp.where(visible, scores, 0.0).astype(jnp.bfloat16)
        local_ref[:, cols] = jnp.dot(weights, v_ref[:, cols], preferred_element_type=jnp.float32)


def _tail_kernel(k_ref, v_ref, dcol_ref, drow_ref, tail_ref):
    count = k_ref.shape[0]
    ending = dcol_ref[...] == drow_ref[...][:, count - 1:count]
    for h, cols in enumerate(head_columns(k_ref)):
        tail_keys = jnp.where(ending, k_ref[:, cols], jnp.zeros((count, HEAD_DIM), k_ref.dtype))
        tail_ref[h] = lax.dot_general(
            tail_keys, v_ref[:, cols], (((0,), (0,)), ((), ())), preferred_element_type=jnp.float32
        )


def _past_kernel(local_ref, q_ref, state_ref, dcol_ref, drow_ref, out_ref):
    joined = dcol_ref[...] == drow_ref[...][:, 0:1]
    for h, cols in enumerate(head_columns(q_ref)):
        from_past = jnp.dot(q_ref[:, cols], state_ref[h], preferred_element_type=jnp.float32)
        out_ref[:, cols] = local_ref[:, cols] + jnp.where(joined, from_past, 0.0)


def head_specs(count, heads, parts):
    return [pl.BlockSpec((count, heads * HEAD_DIM), lambda b, p=p: (b, p)) for p in parts]


def doc_specs(count):
    return [
        pl.BlockSpec((None, count, 1), lambda b: (b, 0, 0)),
        pl.BlockSpec((None, 1, count), lambda b: (b, 0, 0)),
    ]


def state_spec(heads):
    return pl.BlockSpec((None, heads, HEAD_DIM, HEAD_DIM), lambda b: (b, 0, 0, 0))


def local_attention(qkv, docs, heads):
    blocks, count = docs.shape
    return pl.pallas_call(
        _local_kernel,
        grid=(blocks,),
        in_specs=head_specs(count, heads, (0, 1, 2)) + doc_specs(count),
        out_specs=head_specs(count, heads, (0,))[0],
        out_shape=jax.ShapeDtypeStruct((blocks * count, heads * HEAD_DIM), jnp.float32),
    )(qkv, qkv, qkv, docs.reshape(blocks, count, 1), docs.reshape(blocks, 1, count))


def tail_states(qkv, docs, heads):
    blocks, count = docs.shape
    return pl.pallas_call(
        _tail_kernel,
        grid=(blocks,),
        in_specs=head_specs(count, heads, (1, 2)) + doc_specs(count),
        out_specs=state_spec(heads),
        out_shape=jax.ShapeDtypeStruct((blocks, heads, HEAD_DIM, HEAD_DIM), jnp.float32),
    )(qkv, qkv, docs.reshape(blocks, count, 1), docs.reshape(blocks, 1, count))


def add_past(local, qkv, state, docs, heads):
    blocks, count = docs.shape
    tile = head_specs(count, heads, (0,))[0]
    return pl.pallas_call(
        _past_kernel,
        grid=(blocks,),
        in_specs=[tile, tile, state_spec(heads)] + doc_specs(count),
        out_specs=tile,
        out_shape=jax.ShapeDtypeStruct(local.shape, jnp.float32),
        input_output_aliases={0: 0},
    )(local, qkv, state, docs.reshape(blocks, count, 1), docs.reshape(blocks, 1, count))


def make_shards(n_sq, n_fsdp):
    def shards(tokens, doc_ids, norm_gain, query_weight, key_weight, value_weight, out_gain):
        core = lax.axis_index("core")
        sq = lax.axis_index("sq")
        count, width = tokens.shape[1], tokens.shape[2]
        rows = query_weight.shape[0]
        half = ATTN_WIDTH // 2
        heads = HEADS // 2

        normed = norm_rows(tokens[0].astype(jnp.float32), norm_gain).astype(jnp.bfloat16)
        normed = normed.reshape(count, n_sq, 2, n_fsdp, rows).transpose(0, 1, 3, 2, 4)
        normed = normed.reshape(count, width)
        pair = jnp.concatenate([normed, swap_core(normed)], axis=0)

        def halves(start):
            return jnp.concatenate(
                [
                    lax.dynamic_slice_in_dim(weight, start, half, axis=1)
                    for weight in (query_weight, key_weight, value_weight)
                ],
                axis=1,
            )

        mine, other = halves(core * half), halves((1 - core) * half)
        both = in_core_order(core, mine, swap_core(other))
        gathered = lax.all_gather(both, ("sq", "fsdp"), axis=0, tiled=False)
        summed = jnp.dot(pair, gathered.reshape(width, 3 * half), preferred_element_type=jnp.float32)
        qkv = jax.nn.silu(summed).astype(jnp.bfloat16)

        own_docs = doc_ids[0]
        docs = jnp.stack([own_docs, swap_core(own_docs)])
        first, last = docs[:, 0], docs[:, -1]
        slot_core = jnp.stack([core, 1 - core])
        block = 2 * sq + slot_core

        tail = tail_states(qkv, docs, heads)
        local_part = local_attention(qkv, docs, heads)

        tag = jnp.broadcast_to(last.astype(jnp.bfloat16)[:, None, None], (2, 16, HEAD_DIM))
        message = jnp.concatenate([tail.astype(jnp.bfloat16).reshape(2, heads * HEAD_DIM, HEAD_DIM), tag], axis=1)
        received = lax.all_gather(message, "sq")
        all_tail = received[:, :, : heads * HEAD_DIM].reshape(n_sq, 2, heads, HEAD_DIM, HEAD_DIM)
        all_last = received[:, :, heads * HEAD_DIM, 0].astype(jnp.int32)
        all_block = 2 * jnp.arange(n_sq, dtype=jnp.int32)[:, None] + slot_core[None, :]
        counted = (all_block[None] < block[:, None, None]) & (all_last[None] == first[:, None, None])
        carried = jnp.einsum(
            "bsk,skhef->bhef",
            counted.astype(jnp.bfloat16),
            all_tail,
            preferred_element_type=jnp.float32,
        )

        mixed = add_past(local_part, qkv, carried.astype(jnp.bfloat16), docs, heads)
        mixed = mixed.reshape(2, count, half)
        squares = jnp.sum(mixed * mixed, axis=-1)
        total = squares + swap_core(squares)[::-1]
        scale = lax.rsqrt(total / ATTN_WIDTH + EPS)
        gain = lax.dynamic_slice_in_dim(out_gain, core * half, half)
        attended = (mixed * scale[:, :, None] * gain).astype(jnp.bfloat16)
        theirs = swap_core(attended[1])
        out = jnp.where(
            core == 0,
            jnp.concatenate([attended[0], theirs], axis=-1),
            jnp.concatenate([theirs, attended[0]], axis=-1),
        )
        return out[None]

    return shards


def solution(mesh):
    n_seq, n_fsdp = mesh.shape["seq"], mesh.shape["fsdp"]
    chips = Mesh(mesh.devices.reshape(n_seq // 2, 2, n_fsdp), ("sq", "core", "fsdp"))
    seq = ("sq", "core")
    in_specs = (
        P("fsdp", seq, None),
        P("fsdp", seq),
        P(),
        P(("sq", "core", "fsdp"), None),
        P(("sq", "core", "fsdp"), None),
        P(("sq", "core", "fsdp"), None),
        P(),
    )
    out_specs = P("fsdp", seq, None)
    return jax.shard_map(
        make_shards(n_seq // 2, n_fsdp), mesh=chips, in_specs=in_specs, out_specs=out_specs, check_vma=False
    )
```

```python
import jax
import jax.numpy as jnp
from jax import lax
from jax.sharding import Mesh, PartitionSpec as P
from jax.experimental import pallas as pl

HEADS = 12
HEAD_DIM = 128
ATTN_WIDTH = 1536


EPS = 1e-06


def norm_rows(values, gain):
    mean_sq = jnp.mean(values * values, axis=-1, keepdims=True)
    return values * lax.rsqrt(mean_sq + EPS) * gain


def swap_core(value):
    return lax.ppermute(value, "core", [(0, 1), (1, 0)])


def in_core_order(core, mine, theirs):
    return jnp.where(core == 0, jnp.stack([mine, theirs]), jnp.stack([theirs, mine]))


def head_columns(ref):
    return [slice(h * HEAD_DIM, (h + 1) * HEAD_DIM) for h in range(ref.shape[1] // HEAD_DIM)]


def _local_kernel(q_ref, k_ref, v_ref, dcol_ref, drow_ref, local_ref):
    count = q_ref.shape[0]
    row_pos = lax.broadcasted_iota(jnp.int32, (count, count), 0)
    col_pos = lax.broadcasted_iota(jnp.int32, (count, count), 1)
    visible = (row_pos >= col_pos) & (dcol_ref[...] == drow_ref[...])
    for cols in head_columns(q_ref):
        scores = lax.dot_general(
            q_ref[:, cols], k_ref[:, cols], (((1,), (1,)), ((), ())), preferred_element_type=jnp.float32
        )
        weights = jnp.where(visible, scores, 0.0).astype(jnp.bfloat16)
        local_ref[:, cols] = jnp.dot(weights, v_ref[:, cols], preferred_element_type=jnp.float32)


def _tail_kernel(k_ref, v_ref, dcol_ref, drow_ref, tail_ref):
    count = k_ref.shape[0]
    ending = dcol_ref[...] == drow_ref[...][:, count - 1:count]
    for h, cols in enumerate(head_columns(k_ref)):
        tail_keys = jnp.where(ending, k_ref[:, cols], jnp.zeros((count, HEAD_DIM), k_ref.dtype))
        tail_ref[h] = lax.dot_general(
            tail_keys, v_ref[:, cols], (((0,), (0,)), ((), ())), preferred_element_type=jnp.float32
        )


def _past_kernel(local_ref, q_ref, counted_ref, dcol_ref, drow_ref, *rest):
    message_refs, out_ref = rest[:-1], rest[-1]
    joined = dcol_ref[...] == drow_ref[...][:, 0:1]
    for h, cols in enumerate(head_columns(q_ref)):
        carried = jnp.zeros((HEAD_DIM, HEAD_DIM), jnp.float32)
        for shift, message_ref in enumerate(message_refs):
            for slot in range(2):
                part = message_ref[slot, cols, :].astype(jnp.float32)
                carried = carried + counted_ref[2 * shift + slot] * part
        state = carried.astype(jnp.bfloat16)
        from_past = jnp.dot(q_ref[:, cols], state, preferred_element_type=jnp.float32)
        out_ref[:, cols] = local_ref[:, cols] + jnp.where(joined, from_past, 0.0)


def head_specs(count, heads, parts):
    return [pl.BlockSpec((count, heads * HEAD_DIM), lambda b, p=p: (b, p)) for p in parts]


def doc_specs(count):
    return [
        pl.BlockSpec((None, count, 1), lambda b: (b, 0, 0)),
        pl.BlockSpec((None, 1, count), lambda b: (b, 0, 0)),
    ]


def state_spec(heads):
    return pl.BlockSpec((None, heads, HEAD_DIM, HEAD_DIM), lambda b: (b, 0, 0, 0))


def local_attention(qkv, docs, heads):
    blocks, count = docs.shape
    return pl.pallas_call(
        _local_kernel,
        grid=(blocks,),
        in_specs=head_specs(count, heads, (0, 1, 2)) + doc_specs(count),
        out_specs=head_specs(count, heads, (0,))[0],
        out_shape=jax.ShapeDtypeStruct((blocks * count, heads * HEAD_DIM), jnp.float32),
    )(qkv, qkv, qkv, docs.reshape(blocks, count, 1), docs.reshape(blocks, 1, count))


def tail_states(qkv, docs, heads):
    blocks, count = docs.shape
    return pl.pallas_call(
        _tail_kernel,
        grid=(blocks,),
        in_specs=head_specs(count, heads, (1, 2)) + doc_specs(count),
        out_specs=state_spec(heads),
        out_shape=jax.ShapeDtypeStruct((blocks, heads, HEAD_DIM, HEAD_DIM), jnp.float32),
    )(qkv, qkv, docs.reshape(blocks, count, 1), docs.reshape(blocks, 1, count))


def add_past(local, qkv, counted, messages, docs, heads):
    blocks, count = docs.shape
    tile = head_specs(count, heads, (0,))[0]
    sources = counted.shape[1]
    whole = [pl.BlockSpec(message.shape, lambda b: (0, 0, 0)) for message in messages]
    return pl.pallas_call(
        _past_kernel,
        grid=(blocks,),
        in_specs=[tile, tile, pl.BlockSpec((None, sources, 1, HEAD_DIM), lambda b: (b, 0, 0, 0))]
        + doc_specs(count)
        + whole,
        out_specs=tile,
        out_shape=jax.ShapeDtypeStruct(local.shape, jnp.float32),
        input_output_aliases={0: 0},
    )(local, qkv, counted, docs.reshape(blocks, count, 1), docs.reshape(blocks, 1, count), *messages)


def make_shards(n_sq, n_fsdp):
    def shards(tokens, doc_ids, norm_gain, query_weight, key_weight, value_weight, out_gain):
        core = lax.axis_index("core")
        sq = lax.axis_index("sq")
        count, width = tokens.shape[1], tokens.shape[2]
        rows = query_weight.shape[0]
        half = ATTN_WIDTH // 2
        heads = HEADS // 2

        normed = norm_rows(tokens[0].astype(jnp.float32), norm_gain).astype(jnp.bfloat16)
        normed = normed.reshape(count, n_sq, 2, n_fsdp, rows).transpose(0, 1, 3, 2, 4)
        normed = normed.reshape(count, width)
        pair = jnp.concatenate([normed, swap_core(normed)], axis=0)

        def halves(start):
            return jnp.concatenate(
                [
                    lax.dynamic_slice_in_dim(weight, start, half, axis=1)
                    for weight in (query_weight, key_weight, value_weight)
                ],
                axis=1,
            )

        mine, other = halves(core * half), halves((1 - core) * half)
        both = in_core_order(core, mine, swap_core(other))
        gathered = lax.all_gather(both, ("sq", "fsdp"), axis=0, tiled=False)
        summed = jnp.dot(pair, gathered.reshape(width, 3 * half), preferred_element_type=jnp.float32)
        qkv = jax.nn.silu(summed).astype(jnp.bfloat16)

        own_docs = doc_ids[0]
        docs = jnp.stack([own_docs, swap_core(own_docs)])
        first, last = docs[:, 0], docs[:, -1]
        slot_core = jnp.stack([core, 1 - core])
        block = 2 * sq + slot_core

        tail = tail_states(qkv, docs, heads)
        local_part = local_attention(qkv, docs, heads)

        tag = jnp.broadcast_to(last.astype(jnp.bfloat16)[:, None, None], (2, 16, HEAD_DIM))
        message = jnp.concatenate([tail.astype(jnp.bfloat16).reshape(2, heads * HEAD_DIM, HEAD_DIM), tag], axis=1)
        received = [message] + [
            lax.ppermute(message, "sq", [(i, i + shift) for i in range(n_sq - shift)])
            for shift in range(1, n_sq)
        ]
        all_last = jnp.stack([got[:, heads * HEAD_DIM, 0] for got in received]).astype(jnp.int32)
        shifts = jnp.arange(n_sq, dtype=jnp.int32)[:, None]
        all_block = 2 * (sq - shifts) + slot_core[None, :]
        counted = (
            (shifts <= sq)[None]
            & (all_block[None] < block[:, None, None])
            & (all_last[None] == first[:, None, None])
        )
        counted = jnp.broadcast_to(
            counted.reshape(2, 2 * n_sq, 1, 1).astype(jnp.float32), (2, 2 * n_sq, 1, HEAD_DIM)
        )

        mixed = add_past(local_part, qkv, counted, received, docs, heads)
        mixed = mixed.reshape(2, count, half)
        squares = jnp.sum(mixed * mixed, axis=-1)
        total = squares + swap_core(squares)[::-1]
        scale = lax.rsqrt(total / ATTN_WIDTH + EPS)
        gain = lax.dynamic_slice_in_dim(out_gain, core * half, half)
        attended = (mixed * scale[:, :, None] * gain).astype(jnp.bfloat16)
        theirs = swap_core(attended[1])
        out = jnp.where(
            core == 0,
            jnp.concatenate([attended[0], theirs], axis=-1),
            jnp.concatenate([theirs, attended[0]], axis=-1),
        )
        return out[None]

    return shards


def solution(mesh):
    n_seq, n_fsdp = mesh.shape["seq"], mesh.shape["fsdp"]
    chips = Mesh(mesh.devices.reshape(n_seq // 2, 2, n_fsdp), ("sq", "core", "fsdp"))
    seq = ("sq", "core")
    in_specs = (
        P("fsdp", seq, None),
        P("fsdp", seq),
        P(),
        P(("sq", "core", "fsdp"), None),
        P(("sq", "core", "fsdp"), None),
        P(("sq", "core", "fsdp"), None),
        P(),
    )
    out_specs = P("fsdp", seq, None)
    return jax.shard_map(
        make_shards(n_seq // 2, n_fsdp), mesh=chips, in_specs=in_specs, out_specs=out_specs, check_vma=False
    )
```

```python
import jax
import jax.numpy as jnp
from jax import lax
from jax.sharding import Mesh, PartitionSpec as P
from jax.experimental import pallas as pl

HEADS = 12
HEAD_DIM = 128
ATTN_WIDTH = 1536


EPS = 1e-06


def norm_rows(values, gain):
    mean_sq = jnp.mean(values * values, axis=-1, keepdims=True)
    return values * lax.rsqrt(mean_sq + EPS) * gain


def swap_core(value):
    return lax.ppermute(value, "core", [(0, 1), (1, 0)])


def in_core_order(core, mine, theirs):
    return jnp.where(core == 0, jnp.stack([mine, theirs]), jnp.stack([theirs, mine]))


def head_columns(ref):
    return [slice(h * HEAD_DIM, (h + 1) * HEAD_DIM) for h in range(ref.shape[1] // HEAD_DIM)]


def _local_kernel(q_ref, k_ref, v_ref, dcol_ref, drow_ref, local_ref):
    count = q_ref.shape[0]
    row_pos = lax.broadcasted_iota(jnp.int32, (count, count), 0)
    col_pos = lax.broadcasted_iota(jnp.int32, (count, count), 1)
    visible = (row_pos >= col_pos) & (dcol_ref[...] == drow_ref[...])
    for cols in head_columns(q_ref):
        scores = lax.dot_general(
            q_ref[:, cols], k_ref[:, cols], (((1,), (1,)), ((), ())), preferred_element_type=jnp.float32
        )
        weights = jnp.where(visible, scores, 0.0).astype(jnp.bfloat16)
        local_ref[:, cols] = jnp.dot(weights, v_ref[:, cols], preferred_element_type=jnp.float32)


def _tail_kernel(k_ref, v_ref, dcol_ref, drow_ref, tail_ref):
    count = k_ref.shape[0]
    ending = dcol_ref[...] == drow_ref[...][:, count - 1:count]
    for h, cols in enumerate(head_columns(k_ref)):
        tail_keys = jnp.where(ending, k_ref[:, cols], jnp.zeros((count, HEAD_DIM), k_ref.dtype))
        tail_ref[h] = lax.dot_general(
            tail_keys, v_ref[:, cols], (((0,), (0,)), ((), ())), preferred_element_type=jnp.float32
        )


def _past_kernel(local_ref, q_ref, counted_ref, dcol_ref, drow_ref, *rest):
    message_refs, out_ref = rest[:-1], rest[-1]
    joined = dcol_ref[...] == drow_ref[...][:, 0:1]
    for h, cols in enumerate(head_columns(q_ref)):
        carried = jnp.zeros((HEAD_DIM, HEAD_DIM), jnp.float32)
        for shift, message_ref in enumerate(message_refs):
            for slot in range(2):
                part = message_ref[slot, cols, :].astype(jnp.float32)
                carried = carried + counted_ref[2 * shift + slot] * part
        state = carried.astype(jnp.bfloat16)
        from_past = jnp.dot(q_ref[:, cols], state, preferred_element_type=jnp.float32)
        out_ref[:, cols] = local_ref[:, cols] + jnp.where(joined, from_past, 0.0)


def head_specs(count, heads, parts):
    return [pl.BlockSpec((count, heads * HEAD_DIM), lambda b, p=p: (b, p)) for p in parts]


def doc_specs(count):
    return [
        pl.BlockSpec((None, count, 1), lambda b: (b, 0, 0)),
        pl.BlockSpec((None, 1, count), lambda b: (b, 0, 0)),
    ]


def state_spec(heads):
    return pl.BlockSpec((None, heads, HEAD_DIM, HEAD_DIM), lambda b: (b, 0, 0, 0))


def local_attention(qkv, docs, heads):
    blocks, count = docs.shape
    return pl.pallas_call(
        _local_kernel,
        grid=(blocks,),
        in_specs=head_specs(count, heads, (0, 1, 2)) + doc_specs(count),
        out_specs=head_specs(count, heads, (0,))[0],
        out_shape=jax.ShapeDtypeStruct((blocks * count, heads * HEAD_DIM), jnp.float32),
    )(qkv, qkv, qkv, docs.reshape(blocks, count, 1), docs.reshape(blocks, 1, count))


def tail_states(qkv, docs, heads):
    blocks, count = docs.shape
    return pl.pallas_call(
        _tail_kernel,
        grid=(blocks,),
        in_specs=head_specs(count, heads, (1, 2)) + doc_specs(count),
        out_specs=state_spec(heads),
        out_shape=jax.ShapeDtypeStruct((blocks, heads, HEAD_DIM, HEAD_DIM), jnp.float32),
    )(qkv, qkv, docs.reshape(blocks, count, 1), docs.reshape(blocks, 1, count))


def add_past(local, qkv, counted, messages, docs, heads):
    blocks, count = docs.shape
    tile = head_specs(count, heads, (0,))[0]
    sources = counted.shape[1]
    whole = [pl.BlockSpec(message.shape, lambda b: (0, 0, 0)) for message in messages]
    return pl.pallas_call(
        _past_kernel,
        grid=(blocks,),
        in_specs=[tile, tile, pl.BlockSpec((None, sources, 1, HEAD_DIM), lambda b: (b, 0, 0, 0))]
        + doc_specs(count)
        + whole,
        out_specs=tile,
        out_shape=jax.ShapeDtypeStruct(local.shape, jnp.float32),
        input_output_aliases={0: 0},
    )(local, qkv, counted, docs.reshape(blocks, count, 1), docs.reshape(blocks, 1, count), *messages)


def make_shards(n_sq, n_fsdp):
    def shards(tokens, doc_ids, norm_gain, query_weight, key_weight, value_weight, out_gain):
        core = lax.axis_index("core")
        sq = lax.axis_index("sq")
        count, width = tokens.shape[1], tokens.shape[2]
        rows = query_weight.shape[0]
        half = ATTN_WIDTH // 2
        heads = HEADS // 2

        normed = norm_rows(tokens[0].astype(jnp.float32), norm_gain).astype(jnp.bfloat16)
        normed = normed.reshape(count, n_sq, 2, n_fsdp, rows).transpose(0, 1, 3, 2, 4)
        normed = normed.reshape(count, width)
        pair = jnp.concatenate([normed, swap_core(normed)], axis=0)

        def halves(start):
            return jnp.concatenate(
                [
                    lax.dynamic_slice_in_dim(weight, start, half, axis=1)
                    for weight in (query_weight, key_weight, value_weight)
                ],
                axis=1,
            )

        mine, other = halves(core * half), halves((1 - core) * half)
        both = in_core_order(core, mine, swap_core(other))
        gathered = lax.all_gather(both, ("sq", "fsdp"), axis=0, tiled=False)
        summed = jnp.dot(pair, gathered.reshape(width, 3 * half), preferred_element_type=jnp.float32)
        qkv = jax.nn.silu(summed).astype(jnp.bfloat16)

        own_docs = doc_ids[0]
        docs = jnp.stack([own_docs, swap_core(own_docs)])
        first, last = docs[:, 0], docs[:, -1]
        slot_core = jnp.stack([core, 1 - core])
        block = 2 * sq + slot_core

        tail = tail_states(qkv, docs, heads)
        local_part = local_attention(qkv, docs, heads)

        tag = jnp.broadcast_to(last.astype(jnp.bfloat16)[:, None, None], (2, 16, HEAD_DIM))
        message = jnp.concatenate([tail.astype(jnp.bfloat16).reshape(2, heads * HEAD_DIM, HEAD_DIM), tag], axis=1)
        received = [message] + [
            lax.ppermute(message, "sq", [(i, i + shift) for i in range(n_sq - shift)])
            for shift in range(1, n_sq)
        ]
        all_last = jnp.stack([got[:, heads * HEAD_DIM, 0] for got in received]).astype(jnp.int32)
        shifts = jnp.arange(n_sq, dtype=jnp.int32)[:, None]
        all_block = 2 * (sq - shifts) + slot_core[None, :]
        counted = (
            (shifts <= sq)[None]
            & (all_block[None] < block[:, None, None])
            & (all_last[None] == first[:, None, None])
        )
        counted = jnp.broadcast_to(
            counted.reshape(2, 2 * n_sq, 1, 1).astype(jnp.float32), (2, 2 * n_sq, 1, HEAD_DIM)
        )

        mixed = add_past(local_part, qkv, counted, received, docs, heads)
        mixed = mixed.reshape(2, count, half)
        theirs = swap_core(mixed[1])
        full = jnp.where(
            core == 0,
            jnp.concatenate([mixed[0], theirs], axis=-1),
            jnp.concatenate([theirs, mixed[0]], axis=-1),
        )
        out = norm_rows(full, out_gain).astype(jnp.bfloat16)
        return out[None]

    return shards


def solution(mesh):
    n_seq, n_fsdp = mesh.shape["seq"], mesh.shape["fsdp"]
    chips = Mesh(mesh.devices.reshape(n_seq // 2, 2, n_fsdp), ("sq", "core", "fsdp"))
    seq = ("sq", "core")
    in_specs = (
        P("fsdp", seq, None),
        P("fsdp", seq),
        P(),
        P(("sq", "core", "fsdp"), None),
        P(("sq", "core", "fsdp"), None),
        P(("sq", "core", "fsdp"), None),
        P(),
    )
    out_specs = P("fsdp", seq, None)
    return jax.shard_map(
        make_shards(n_seq // 2, n_fsdp), mesh=chips, in_specs=in_specs, out_specs=out_specs, check_vma=False
    )
```

```python
import jax
import jax.numpy as jnp
from jax import lax
from jax.sharding import Mesh, PartitionSpec as P
from jax.experimental import pallas as pl

HEADS = 12
HEAD_DIM = 128
ATTN_WIDTH = 1536


EPS = 1e-06


def norm_rows(values, gain):
    mean_sq = jnp.mean(values * values, axis=-1, keepdims=True)
    return values * lax.rsqrt(mean_sq + EPS) * gain


def swap_core(value):
    return lax.ppermute(value, "core", [(0, 1), (1, 0)])


def in_core_order(core, mine, theirs):
    return jnp.where(core == 0, jnp.stack([mine, theirs]), jnp.stack([theirs, mine]))


def head_columns(ref):
    return [slice(h * HEAD_DIM, (h + 1) * HEAD_DIM) for h in range(ref.shape[1] // HEAD_DIM)]


def _local_kernel(q_ref, k_ref, v_ref, dcol_ref, drow_ref, local_ref):
    count = q_ref.shape[0]
    row_pos = lax.broadcasted_iota(jnp.int32, (count, count), 0)
    col_pos = lax.broadcasted_iota(jnp.int32, (count, count), 1)
    visible = (row_pos >= col_pos) & (dcol_ref[...] == drow_ref[...])
    for cols in head_columns(q_ref):
        scores = lax.dot_general(
            q_ref[:, cols], k_ref[:, cols], (((1,), (1,)), ((), ())), preferred_element_type=jnp.float32
        )
        weights = jnp.where(visible, scores, 0.0).astype(jnp.bfloat16)
        local_ref[:, cols] = jnp.dot(weights, v_ref[:, cols], preferred_element_type=jnp.float32)


def _tail_kernel(k_ref, v_ref, dcol_ref, drow_ref, tail_ref):
    count = k_ref.shape[0]
    ending = dcol_ref[...] == drow_ref[...][:, count - 1:count]
    for h, cols in enumerate(head_columns(k_ref)):
        tail_keys = jnp.where(ending, k_ref[:, cols], jnp.zeros((count, HEAD_DIM), k_ref.dtype))
        tail_ref[h] = lax.dot_general(
            tail_keys, v_ref[:, cols], (((0,), (0,)), ((), ())), preferred_element_type=jnp.float32
        )


def _past_kernel(local_ref, q_ref, counted_ref, dcol_ref, drow_ref, *rest):
    message_refs, out_ref = rest[:-1], rest[-1]
    joined = dcol_ref[...] == drow_ref[...][:, 0:1]
    for h, cols in enumerate(head_columns(q_ref)):
        carried = jnp.zeros((HEAD_DIM, HEAD_DIM), jnp.float32)
        index = 0
        for message_ref in message_refs:
            for slot in range(message_ref.shape[0]):
                part = message_ref[slot, cols, :].astype(jnp.float32)
                carried = carried + counted_ref[index] * part
                index += 1
        state = carried.astype(jnp.bfloat16)
        from_past = jnp.dot(q_ref[:, cols], state, preferred_element_type=jnp.float32)
        out_ref[:, cols] = local_ref[:, cols] + jnp.where(joined, from_past, 0.0)


def head_specs(count, heads, parts):
    return [pl.BlockSpec((count, heads * HEAD_DIM), lambda b, p=p: (b, p)) for p in parts]


def doc_specs(count):
    return [
        pl.BlockSpec((None, count, 1), lambda b: (b, 0, 0)),
        pl.BlockSpec((None, 1, count), lambda b: (b, 0, 0)),
    ]


def state_spec(heads):
    return pl.BlockSpec((None, heads, HEAD_DIM, HEAD_DIM), lambda b: (b, 0, 0, 0))


def local_attention(qkv, docs, heads):
    blocks, count = docs.shape
    return pl.pallas_call(
        _local_kernel,
        grid=(blocks,),
        in_specs=head_specs(count, heads, (0, 1, 2)) + doc_specs(count),
        out_specs=head_specs(count, heads, (0,))[0],
        out_shape=jax.ShapeDtypeStruct((blocks * count, heads * HEAD_DIM), jnp.float32),
    )(qkv, qkv, qkv, docs.reshape(blocks, count, 1), docs.reshape(blocks, 1, count))


def tail_states(qkv, docs, heads):
    blocks, count = docs.shape
    return pl.pallas_call(
        _tail_kernel,
        grid=(blocks,),
        in_specs=head_specs(count, heads, (1, 2)) + doc_specs(count),
        out_specs=state_spec(heads),
        out_shape=jax.ShapeDtypeStruct((blocks, heads, HEAD_DIM, HEAD_DIM), jnp.float32),
    )(qkv, qkv, docs.reshape(blocks, count, 1), docs.reshape(blocks, 1, count))


def add_past(local, qkv, counted, messages, docs, heads):
    blocks, count = docs.shape
    tile = head_specs(count, heads, (0,))[0]
    sources = counted.shape[1]
    whole = [pl.BlockSpec(message.shape, lambda b: (0, 0, 0)) for message in messages]
    return pl.pallas_call(
        _past_kernel,
        grid=(blocks,),
        in_specs=[tile, tile, pl.BlockSpec((None, sources, 1, HEAD_DIM), lambda b: (b, 0, 0, 0))]
        + doc_specs(count)
        + whole,
        out_specs=tile,
        out_shape=jax.ShapeDtypeStruct(local.shape, jnp.float32),
        input_output_aliases={0: 0},
    )(local, qkv, counted, docs.reshape(blocks, count, 1), docs.reshape(blocks, 1, count), *messages)


def make_shards(n_sq, n_fsdp):
    def shards(tokens, doc_ids, norm_gain, query_weight, key_weight, value_weight, out_gain):
        core = lax.axis_index("core")
        sq = lax.axis_index("sq")
        count, width = tokens.shape[1], tokens.shape[2]
        rows = query_weight.shape[0]
        half = ATTN_WIDTH // 2
        heads = HEADS // 2

        normed = norm_rows(tokens[0].astype(jnp.float32), norm_gain).astype(jnp.bfloat16)
        normed = normed.reshape(count, n_sq, 2, n_fsdp, rows).transpose(0, 1, 3, 2, 4)
        normed = normed.reshape(count, width)
        pair = jnp.concatenate([normed, swap_core(normed)], axis=0)

        def halves(start):
            return jnp.concatenate(
                [
                    lax.dynamic_slice_in_dim(weight, start, half, axis=1)
                    for weight in (query_weight, key_weight, value_weight)
                ],
                axis=1,
            )

        mine, other = halves(core * half), halves((1 - core) * half)
        both = in_core_order(core, mine, swap_core(other))
        gathered = lax.all_gather(both, ("sq", "fsdp"), axis=0, tiled=False)
        summed = jnp.dot(pair, gathered.reshape(width, 3 * half), preferred_element_type=jnp.float32)
        qkv = jax.nn.silu(summed).astype(jnp.bfloat16)

        own_docs = doc_ids[0]
        docs = jnp.stack([own_docs, swap_core(own_docs)])
        first, last = docs[:, 0], docs[:, -1]
        slot_core = jnp.stack([core, 1 - core])
        block = 2 * sq + slot_core

        tail = tail_states(qkv, docs, heads)
        local_part = local_attention(qkv, docs, heads)

        own_message = tail.astype(jnp.bfloat16).reshape(2, heads * HEAD_DIM, HEAD_DIM)
        own_counted = (block[None, :] < block[:, None]) & (last[None, :] == first[:, None])
        first_tail, second_tail = jnp.where(core == 0, tail[0], tail[1]), jnp.where(core == 0, tail[1], tail[0])
        first_last, second_last = jnp.where(core == 0, last[0], last[1]), jnp.where(core == 0, last[1], last[0])
        chip_tail = second_tail + jnp.where(first_last == second_last, first_tail, 0.0)
        tag = jnp.broadcast_to(second_last.astype(jnp.bfloat16), (1, 16, HEAD_DIM))
        message = jnp.concatenate(
            [chip_tail.astype(jnp.bfloat16).reshape(1, heads * HEAD_DIM, HEAD_DIM), tag], axis=1
        )
        received = [
            lax.ppermute(message, "sq", [(i, i + shift) for i in range(n_sq - shift)])
            for shift in range(1, n_sq)
        ]
        chip_last = jnp.stack([got[0, heads * HEAD_DIM, 0] for got in received]).astype(jnp.int32)
        shifts = jnp.arange(1, n_sq, dtype=jnp.int32)
        far_counted = (shifts <= sq)[None, :] & (chip_last[None, :] == first[:, None])
        counted = jnp.concatenate([own_counted, far_counted], axis=1)
        counted = jnp.broadcast_to(
            counted.reshape(2, n_sq + 1, 1, 1).astype(jnp.float32), (2, n_sq + 1, 1, HEAD_DIM)
        )

        mixed = add_past(local_part, qkv, counted, [own_message] + received, docs, heads)
        mixed = mixed.reshape(2, count, half)
        squares = jnp.sum(mixed * mixed, axis=-1)
        total = squares + swap_core(squares)[::-1]
        scale = lax.rsqrt(total / ATTN_WIDTH + EPS)
        gain = lax.dynamic_slice_in_dim(out_gain, core * half, half)
        attended = (mixed * scale[:, :, None] * gain).astype(jnp.bfloat16)
        theirs = swap_core(attended[1])
        out = jnp.where(
            core == 0,
            jnp.concatenate([attended[0], theirs], axis=-1),
            jnp.concatenate([theirs, attended[0]], axis=-1),
        )
        return out[None]

    return shards


def solution(mesh):
    n_seq, n_fsdp = mesh.shape["seq"], mesh.shape["fsdp"]
    chips = Mesh(mesh.devices.reshape(n_seq // 2, 2, n_fsdp), ("sq", "core", "fsdp"))
    seq = ("sq", "core")
    in_specs = (
        P("fsdp", seq, None),
        P("fsdp", seq),
        P(),
        P(("sq", "core", "fsdp"), None),
        P(("sq", "core", "fsdp"), None),
        P(("sq", "core", "fsdp"), None),
        P(),
    )
    out_specs = P("fsdp", seq, None)
    return jax.shard_map(
        make_shards(n_seq // 2, n_fsdp), mesh=chips, in_specs=in_specs, out_specs=out_specs, check_vma=False
    )
```

```python
import jax
import jax.numpy as jnp
from jax import lax
from jax.sharding import Mesh, PartitionSpec as P
from jax.experimental import pallas as pl

HEADS = 12
HEAD_DIM = 128
ATTN_WIDTH = 1536


EPS = 1e-06


def norm_rows(values, gain):
    mean_sq = jnp.mean(values * values, axis=-1, keepdims=True)
    return values * lax.rsqrt(mean_sq + EPS) * gain


def swap_core(value):
    return lax.ppermute(value, "core", [(0, 1), (1, 0)])


def in_core_order(core, mine, theirs):
    return jnp.where(core == 0, jnp.stack([mine, theirs]), jnp.stack([theirs, mine]))


def head_columns(ref):
    return [slice(h * HEAD_DIM, (h + 1) * HEAD_DIM) for h in range(ref.shape[1] // HEAD_DIM)]


def _local_kernel(q_ref, k_ref, v_ref, dcol_ref, drow_ref, local_ref):
    count = q_ref.shape[0]
    row_pos = lax.broadcasted_iota(jnp.int32, (count, count), 0)
    col_pos = lax.broadcasted_iota(jnp.int32, (count, count), 1)
    visible = (row_pos >= col_pos) & (dcol_ref[...] == drow_ref[...])
    for cols in head_columns(q_ref):
        scores = lax.dot_general(
            q_ref[:, cols], k_ref[:, cols], (((1,), (1,)), ((), ())), preferred_element_type=jnp.float32
        )
        weights = jnp.where(visible, scores, 0.0).astype(jnp.bfloat16)
        local_ref[:, cols] = jnp.dot(weights, v_ref[:, cols], preferred_element_type=jnp.float32)


def _tail_kernel(k_ref, v_ref, dcol_ref, drow_ref, own_ref, message_ref):
    count = dcol_ref.shape[1]
    lasts = [drow_ref[block][:, count - 1:count] for block in range(2)]
    chip_last = jnp.maximum(lasts[0], lasts[1])
    for h, cols in enumerate(head_columns(k_ref)):
        chip = jnp.zeros((HEAD_DIM, HEAD_DIM), jnp.float32)
        for block in range(2):
            rows = slice(block * count, (block + 1) * count)
            ending = dcol_ref[block] == lasts[block]
            tail_keys = jnp.where(ending, k_ref[rows, cols], jnp.zeros((count, HEAD_DIM), k_ref.dtype))
            tail = lax.dot_general(
                tail_keys, v_ref[rows, cols], (((0,), (0,)), ((), ())), preferred_element_type=jnp.float32
            )
            own_ref[block, cols, :] = tail.astype(jnp.bfloat16)
            chip = chip + jnp.where(lasts[block] == chip_last, tail, 0.0)
        message_ref[0, cols, :] = chip.astype(jnp.bfloat16)
    tag = jnp.broadcast_to(chip_last.astype(jnp.float32), (16, HEAD_DIM)).astype(jnp.bfloat16)
    message_ref[0, pl.ds(k_ref.shape[1], 16), :] = tag


def _past_kernel(local_ref, q_ref, counted_ref, dcol_ref, drow_ref, *rest):
    message_refs, out_ref = rest[:-1], rest[-1]
    joined = dcol_ref[...] == drow_ref[...][:, 0:1]
    for h, cols in enumerate(head_columns(q_ref)):
        carried = jnp.zeros((HEAD_DIM, HEAD_DIM), jnp.float32)
        index = 0
        for message_ref in message_refs:
            for slot in range(message_ref.shape[0]):
                part = message_ref[slot, cols, :].astype(jnp.float32)
                carried = carried + counted_ref[index] * part
                index += 1
        state = carried.astype(jnp.bfloat16)
        from_past = jnp.dot(q_ref[:, cols], state, preferred_element_type=jnp.float32)
        out_ref[:, cols] = local_ref[:, cols] + jnp.where(joined, from_past, 0.0)


def head_specs(count, heads, parts):
    return [pl.BlockSpec((count, heads * HEAD_DIM), lambda b, p=p: (b, p)) for p in parts]


def doc_specs(count):
    return [
        pl.BlockSpec((None, count, 1), lambda b: (b, 0, 0)),
        pl.BlockSpec((None, 1, count), lambda b: (b, 0, 0)),
    ]


def state_spec(heads):
    return pl.BlockSpec((None, heads, HEAD_DIM, HEAD_DIM), lambda b: (b, 0, 0, 0))


def local_attention(qkv, docs, heads):
    blocks, count = docs.shape
    return pl.pallas_call(
        _local_kernel,
        grid=(blocks,),
        in_specs=head_specs(count, heads, (0, 1, 2)) + doc_specs(count),
        out_specs=head_specs(count, heads, (0,))[0],
        out_shape=jax.ShapeDtypeStruct((blocks * count, heads * HEAD_DIM), jnp.float32),
    )(qkv, qkv, qkv, docs.reshape(blocks, count, 1), docs.reshape(blocks, 1, count))


def tail_states(qkv, docs, heads):
    blocks, count = docs.shape
    width = heads * HEAD_DIM
    return pl.pallas_call(
        _tail_kernel,
        grid=(1,),
        in_specs=[
            pl.BlockSpec((blocks * count, width), lambda i: (0, 1)),
            pl.BlockSpec((blocks * count, width), lambda i: (0, 2)),
            pl.BlockSpec((blocks, count, 1), lambda i: (0, 0, 0)),
            pl.BlockSpec((blocks, 1, count), lambda i: (0, 0, 0)),
        ],
        out_specs=[
            pl.BlockSpec((blocks, width, HEAD_DIM), lambda i: (0, 0, 0)),
            pl.BlockSpec((1, width + 16, HEAD_DIM), lambda i: (0, 0, 0)),
        ],
        out_shape=[
            jax.ShapeDtypeStruct((blocks, width, HEAD_DIM), jnp.bfloat16),
            jax.ShapeDtypeStruct((1, width + 16, HEAD_DIM), jnp.bfloat16),
        ],
    )(qkv, qkv, docs.reshape(blocks, count, 1), docs.reshape(blocks, 1, count))


def add_past(local, qkv, counted, messages, docs, heads):
    blocks, count = docs.shape
    tile = head_specs(count, heads, (0,))[0]
    sources = counted.shape[1]
    whole = [pl.BlockSpec(message.shape, lambda b: (0, 0, 0)) for message in messages]
    return pl.pallas_call(
        _past_kernel,
        grid=(blocks,),
        in_specs=[tile, tile, pl.BlockSpec((None, sources, 1, HEAD_DIM), lambda b: (b, 0, 0, 0))]
        + doc_specs(count)
        + whole,
        out_specs=tile,
        out_shape=jax.ShapeDtypeStruct(local.shape, jnp.float32),
        input_output_aliases={0: 0},
    )(local, qkv, counted, docs.reshape(blocks, count, 1), docs.reshape(blocks, 1, count), *messages)


def make_shards(n_sq, n_fsdp):
    def shards(tokens, doc_ids, norm_gain, query_weight, key_weight, value_weight, out_gain):
        core = lax.axis_index("core")
        sq = lax.axis_index("sq")
        count, width = tokens.shape[1], tokens.shape[2]
        rows = query_weight.shape[0]
        half = ATTN_WIDTH // 2
        heads = HEADS // 2

        normed = norm_rows(tokens[0].astype(jnp.float32), norm_gain).astype(jnp.bfloat16)
        normed = normed.reshape(count, n_sq, 2, n_fsdp, rows).transpose(0, 1, 3, 2, 4)
        normed = normed.reshape(count, width)
        pair = jnp.concatenate([normed, swap_core(normed)], axis=0)

        def halves(start):
            return jnp.concatenate(
                [
                    lax.dynamic_slice_in_dim(weight, start, half, axis=1)
                    for weight in (query_weight, key_weight, value_weight)
                ],
                axis=1,
            )

        mine, other = halves(core * half), halves((1 - core) * half)
        both = in_core_order(core, mine, swap_core(other))
        gathered = lax.all_gather(both, ("sq", "fsdp"), axis=0, tiled=False)
        summed = jnp.dot(pair, gathered.reshape(width, 3 * half), preferred_element_type=jnp.float32)
        qkv = jax.nn.silu(summed).astype(jnp.bfloat16)

        own_docs = doc_ids[0]
        docs = jnp.stack([own_docs, swap_core(own_docs)])
        first, last = docs[:, 0], docs[:, -1]
        slot_core = jnp.stack([core, 1 - core])
        block = 2 * sq + slot_core

        own_message, message = tail_states(qkv, docs, heads)
        local_part = local_attention(qkv, docs, heads)

        own_counted = (block[None, :] < block[:, None]) & (last[None, :] == first[:, None])
        received = [
            lax.ppermute(message, "sq", [(i, i + shift) for i in range(n_sq - shift)])
            for shift in range(1, n_sq)
        ]
        chip_last = jnp.stack([got[0, heads * HEAD_DIM, 0] for got in received]).astype(jnp.int32)
        shifts = jnp.arange(1, n_sq, dtype=jnp.int32)
        far_counted = (shifts <= sq)[None, :] & (chip_last[None, :] == first[:, None])
        counted = jnp.concatenate([own_counted, far_counted], axis=1)
        counted = jnp.broadcast_to(
            counted.reshape(2, n_sq + 1, 1, 1).astype(jnp.float32), (2, n_sq + 1, 1, HEAD_DIM)
        )

        mixed = add_past(local_part, qkv, counted, [own_message] + received, docs, heads)
        mixed = mixed.reshape(2, count, half)
        squares = jnp.sum(mixed * mixed, axis=-1)
        total = squares + swap_core(squares)[::-1]
        scale = lax.rsqrt(total / ATTN_WIDTH + EPS)
        gain = lax.dynamic_slice_in_dim(out_gain, core * half, half)
        attended = (mixed * scale[:, :, None] * gain).astype(jnp.bfloat16)
        theirs = swap_core(attended[1])
        out = jnp.where(
            core == 0,
            jnp.concatenate([attended[0], theirs], axis=-1),
            jnp.concatenate([theirs, attended[0]], axis=-1),
        )
        return out[None]

    return shards


def solution(mesh):
    n_seq, n_fsdp = mesh.shape["seq"], mesh.shape["fsdp"]
    chips = Mesh(mesh.devices.reshape(n_seq // 2, 2, n_fsdp), ("sq", "core", "fsdp"))
    seq = ("sq", "core")
    in_specs = (
        P("fsdp", seq, None),
        P("fsdp", seq),
        P(),
        P(("sq", "core", "fsdp"), None),
        P(("sq", "core", "fsdp"), None),
        P(("sq", "core", "fsdp"), None),
        P(),
    )
    out_specs = P("fsdp", seq, None)
    return jax.shard_map(
        make_shards(n_seq // 2, n_fsdp), mesh=chips, in_specs=in_specs, out_specs=out_specs, check_vma=False
    )
```

```python
import jax
import jax.numpy as jnp
from jax import lax
from jax.sharding import Mesh, PartitionSpec as P
from jax.experimental import pallas as pl

HEADS = 12
HEAD_DIM = 128
ATTN_WIDTH = 1536


EPS = 1e-06


def norm_rows(values, gain):
    mean_sq = jnp.mean(values * values, axis=-1, keepdims=True)
    return values * lax.rsqrt(mean_sq + EPS) * gain


def swap_core(value):
    return lax.ppermute(value, "core", [(0, 1), (1, 0)])


def in_core_order(core, mine, theirs):
    return jnp.where(core == 0, jnp.stack([mine, theirs]), jnp.stack([theirs, mine]))


def head_columns(ref):
    return [slice(h * HEAD_DIM, (h + 1) * HEAD_DIM) for h in range(ref.shape[1] // HEAD_DIM)]


def _local_kernel(q_ref, k_ref, v_ref, dcol_ref, drow_ref, local_ref):
    count = q_ref.shape[0]
    row_pos = lax.broadcasted_iota(jnp.int32, (count, count), 0)
    col_pos = lax.broadcasted_iota(jnp.int32, (count, count), 1)
    visible = (row_pos >= col_pos) & (dcol_ref[...] == drow_ref[...])
    for cols in head_columns(q_ref):
        scores = lax.dot_general(
            q_ref[:, cols], k_ref[:, cols], (((1,), (1,)), ((), ())), preferred_element_type=jnp.float32
        )
        weights = jnp.where(visible, scores, 0.0).astype(jnp.bfloat16)
        local_ref[:, cols] = jnp.dot(weights, v_ref[:, cols], preferred_element_type=jnp.float32)


def _tail_kernel(k_ref, v_ref, dcol_ref, drow_ref, own_ref, message_ref):
    count = dcol_ref.shape[1]
    lasts = [drow_ref[block][:, count - 1:count] for block in range(2)]
    chip_last = jnp.maximum(lasts[0], lasts[1])
    for h, cols in enumerate(head_columns(k_ref)):
        chip = jnp.zeros((HEAD_DIM, HEAD_DIM), jnp.float32)
        for block in range(2):
            rows = slice(block * count, (block + 1) * count)
            ending = dcol_ref[block] == lasts[block]
            tail_keys = jnp.where(ending, k_ref[rows, cols], jnp.zeros((count, HEAD_DIM), k_ref.dtype))
            tail = lax.dot_general(
                tail_keys, v_ref[rows, cols], (((0,), (0,)), ((), ())), preferred_element_type=jnp.float32
            )
            own_ref[block, cols, :] = tail.astype(jnp.bfloat16)
            chip = chip + jnp.where(lasts[block] == chip_last, tail, 0.0)
        message_ref[0, cols, :] = chip.astype(jnp.bfloat16)
    tag = jnp.broadcast_to(chip_last.astype(jnp.float32), (16, HEAD_DIM)).astype(jnp.bfloat16)
    message_ref[0, pl.ds(k_ref.shape[1], 16), :] = tag


def _past_kernel(local_ref, q_ref, counted_ref, dcol_ref, drow_ref, *rest):
    message_refs, out_ref = rest[:-1], rest[-1]
    joined = dcol_ref[...] == drow_ref[...][:, 0:1]
    for h, cols in enumerate(head_columns(q_ref)):
        carried = jnp.zeros((HEAD_DIM, HEAD_DIM), jnp.float32)
        index = 0
        for message_ref in message_refs:
            for slot in range(message_ref.shape[0]):
                part = message_ref[slot, cols, :].astype(jnp.float32)
                carried = carried + counted_ref[index] * part
                index += 1
        state = carried.astype(jnp.bfloat16)
        from_past = jnp.dot(q_ref[:, cols], state, preferred_element_type=jnp.float32)
        out_ref[:, cols] = local_ref[:, cols] + jnp.where(joined, from_past, 0.0)


def head_specs(count, heads, parts):
    return [pl.BlockSpec((count, heads * HEAD_DIM), lambda b, p=p: (b, p)) for p in parts]


def doc_specs(count):
    return [
        pl.BlockSpec((None, count, 1), lambda b: (b, 0, 0)),
        pl.BlockSpec((None, 1, count), lambda b: (b, 0, 0)),
    ]


def state_spec(heads):
    return pl.BlockSpec((None, heads, HEAD_DIM, HEAD_DIM), lambda b: (b, 0, 0, 0))


def local_attention(qkv, docs, heads):
    blocks, count = docs.shape
    return pl.pallas_call(
        _local_kernel,
        grid=(blocks,),
        in_specs=head_specs(count, heads, (0, 1, 2)) + doc_specs(count),
        out_specs=head_specs(count, heads, (0,))[0],
        out_shape=jax.ShapeDtypeStruct((blocks * count, heads * HEAD_DIM), jnp.float32),
    )(qkv, qkv, qkv, docs.reshape(blocks, count, 1), docs.reshape(blocks, 1, count))


def tail_states(qkv, docs, heads):
    blocks, count = docs.shape
    width = heads * HEAD_DIM
    return pl.pallas_call(
        _tail_kernel,
        grid=(1,),
        in_specs=[
            pl.BlockSpec((blocks * count, width), lambda i: (0, 1)),
            pl.BlockSpec((blocks * count, width), lambda i: (0, 2)),
            pl.BlockSpec((blocks, count, 1), lambda i: (0, 0, 0)),
            pl.BlockSpec((blocks, 1, count), lambda i: (0, 0, 0)),
        ],
        out_specs=[
            pl.BlockSpec((blocks, width, HEAD_DIM), lambda i: (0, 0, 0)),
            pl.BlockSpec((1, width + 16, HEAD_DIM), lambda i: (0, 0, 0)),
        ],
        out_shape=[
            jax.ShapeDtypeStruct((blocks, width, HEAD_DIM), jnp.bfloat16),
            jax.ShapeDtypeStruct((1, width + 16, HEAD_DIM), jnp.bfloat16),
        ],
    )(qkv, qkv, docs.reshape(blocks, count, 1), docs.reshape(blocks, 1, count))


def add_past(local, qkv, counted, messages, docs, heads):
    blocks, count = docs.shape
    tile = head_specs(count, heads, (0,))[0]
    sources = counted.shape[1]
    whole = [pl.BlockSpec(message.shape, lambda b: (0, 0, 0)) for message in messages]
    return pl.pallas_call(
        _past_kernel,
        grid=(blocks,),
        in_specs=[tile, tile, pl.BlockSpec((None, sources, 1, HEAD_DIM), lambda b: (b, 0, 0, 0))]
        + doc_specs(count)
        + whole,
        out_specs=tile,
        out_shape=jax.ShapeDtypeStruct(local.shape, jnp.float32),
        input_output_aliases={0: 0},
    )(local, qkv, counted, docs.reshape(blocks, count, 1), docs.reshape(blocks, 1, count), *messages)


def make_shards(n_sq, n_fsdp):
    def shards(tokens, doc_ids, norm_gain, query_weight, key_weight, value_weight, out_gain):
        core = lax.axis_index("core")
        sq = lax.axis_index("sq")
        count, width = tokens.shape[1], tokens.shape[2]
        rows = query_weight.shape[0]
        half = ATTN_WIDTH // 2
        heads = HEADS // 2

        normed = norm_rows(tokens[0].astype(jnp.float32), norm_gain).astype(jnp.bfloat16)
        normed = normed.reshape(count, n_sq, 2, n_fsdp, rows).transpose(0, 1, 3, 2, 4)
        normed = normed.reshape(count, width)
        pair = jnp.concatenate([normed, swap_core(normed)], axis=0)

        own_docs = doc_ids[0]
        docs = jnp.stack([own_docs, swap_core(own_docs)])
        first, last = docs[:, 0], docs[:, -1]
        chip_last = jnp.stack(
            [
                lax.ppermute(jnp.max(last), "sq", [(i, i + shift) for i in range(n_sq - shift)])
                for shift in range(1, n_sq)
            ]
        )
        pair, chip_last = lax.optimization_barrier((pair, chip_last))

        def halves(start):
            return jnp.concatenate(
                [
                    lax.dynamic_slice_in_dim(weight, start, half, axis=1)
                    for weight in (query_weight, key_weight, value_weight)
                ],
                axis=1,
            )

        mine, other = halves(core * half), halves((1 - core) * half)
        both = in_core_order(core, mine, swap_core(other))
        gathered = lax.all_gather(both, ("sq", "fsdp"), axis=0, tiled=False)
        summed = jnp.dot(pair, gathered.reshape(width, 3 * half), preferred_element_type=jnp.float32)
        qkv = jax.nn.silu(summed).astype(jnp.bfloat16)

        slot_core = jnp.stack([core, 1 - core])
        block = 2 * sq + slot_core

        own_message, message = tail_states(qkv, docs, heads)
        local_part = local_attention(qkv, docs, heads)

        own_counted = (block[None, :] < block[:, None]) & (last[None, :] == first[:, None])
        received = [
            lax.ppermute(message, "sq", [(i, i + shift) for i in range(n_sq - shift)])
            for shift in range(1, n_sq)
        ]
        shifts = jnp.arange(1, n_sq, dtype=jnp.int32)
        far_counted = (shifts <= sq)[None, :] & (chip_last[None, :] == first[:, None])
        counted = jnp.concatenate([own_counted, far_counted], axis=1)
        counted = jnp.broadcast_to(
            counted.reshape(2, n_sq + 1, 1, 1).astype(jnp.float32), (2, n_sq + 1, 1, HEAD_DIM)
        )

        mixed = add_past(local_part, qkv, counted, [own_message] + received, docs, heads)
        mixed = mixed.reshape(2, count, half)
        squares = jnp.sum(mixed * mixed, axis=-1)
        total = squares + swap_core(squares)[::-1]
        scale = lax.rsqrt(total / ATTN_WIDTH + EPS)
        gain = lax.dynamic_slice_in_dim(out_gain, core * half, half)
        attended = (mixed * scale[:, :, None] * gain).astype(jnp.bfloat16)
        theirs = swap_core(attended[1])
        out = jnp.where(
            core == 0,
            jnp.concatenate([attended[0], theirs], axis=-1),
            jnp.concatenate([theirs, attended[0]], axis=-1),
        )
        return out[None]

    return shards


def solution(mesh):
    n_seq, n_fsdp = mesh.shape["seq"], mesh.shape["fsdp"]
    chips = Mesh(mesh.devices.reshape(n_seq // 2, 2, n_fsdp), ("sq", "core", "fsdp"))
    seq = ("sq", "core")
    in_specs = (
        P("fsdp", seq, None),
        P("fsdp", seq),
        P(),
        P(("sq", "core", "fsdp"), None),
        P(("sq", "core", "fsdp"), None),
        P(("sq", "core", "fsdp"), None),
        P(),
    )
    out_specs = P("fsdp", seq, None)
    return jax.shard_map(
        make_shards(n_seq // 2, n_fsdp), mesh=chips, in_specs=in_specs, out_specs=out_specs, check_vma=False
    )
```

```python
import jax
import jax.numpy as jnp
from jax import lax
from jax.sharding import Mesh, PartitionSpec as P
from jax.experimental import pallas as pl

HEADS = 12
HEAD_DIM = 128
ATTN_WIDTH = 1536


EPS = 1e-06


def norm_rows(values, gain):
    mean_sq = jnp.mean(values * values, axis=-1, keepdims=True)
    return values * lax.rsqrt(mean_sq + EPS) * gain


def swap_core(value):
    return lax.ppermute(value, "core", [(0, 1), (1, 0)])


def in_core_order(core, mine, theirs):
    return jnp.where(core == 0, jnp.stack([mine, theirs]), jnp.stack([theirs, mine]))


def head_columns(ref):
    return [slice(h * HEAD_DIM, (h + 1) * HEAD_DIM) for h in range(ref.shape[1] // HEAD_DIM)]


def _local_kernel(q_ref, k_ref, v_ref, dcol_ref, drow_ref, local_ref):
    count = q_ref.shape[0]
    row_pos = lax.broadcasted_iota(jnp.int32, (count, count), 0)
    col_pos = lax.broadcasted_iota(jnp.int32, (count, count), 1)
    visible = (row_pos >= col_pos) & (dcol_ref[...] == drow_ref[...])
    for cols in head_columns(q_ref):
        scores = lax.dot_general(
            q_ref[:, cols], k_ref[:, cols], (((1,), (1,)), ((), ())), preferred_element_type=jnp.float32
        )
        weights = jnp.where(visible, scores, 0.0).astype(jnp.bfloat16)
        local_ref[:, cols] = jnp.dot(weights, v_ref[:, cols], preferred_element_type=jnp.float32)


def _tail_kernel(k_ref, v_ref, dcol_ref, drow_ref, own_ref, message_ref):
    count = dcol_ref.shape[1]
    lasts = [drow_ref[block][:, count - 1:count] for block in range(2)]
    chip_last = jnp.maximum(lasts[0], lasts[1])
    for h, cols in enumerate(head_columns(k_ref)):
        chip = jnp.zeros((HEAD_DIM, HEAD_DIM), jnp.float32)
        for block in range(2):
            rows = slice(block * count, (block + 1) * count)
            ending = dcol_ref[block] == lasts[block]
            tail_keys = jnp.where(ending, k_ref[rows, cols], jnp.zeros((count, HEAD_DIM), k_ref.dtype))
            tail = lax.dot_general(
                tail_keys, v_ref[rows, cols], (((0,), (0,)), ((), ())), preferred_element_type=jnp.float32
            )
            own_ref[block, cols, :] = tail.astype(jnp.bfloat16)
            chip = chip + jnp.where(lasts[block] == chip_last, tail, 0.0)
        message_ref[0, cols, :] = chip.astype(jnp.bfloat16)
    tag = jnp.broadcast_to(chip_last.astype(jnp.float32), (16, HEAD_DIM)).astype(jnp.bfloat16)
    message_ref[0, pl.ds(k_ref.shape[1], 16), :] = tag


def _past_kernel(local_ref, q_ref, counted_ref, dcol_ref, drow_ref, *rest):
    message_refs, out_ref = rest[:-1], rest[-1]
    joined = dcol_ref[...] == drow_ref[...][:, 0:1]
    for h, cols in enumerate(head_columns(q_ref)):
        carried = jnp.zeros((HEAD_DIM, HEAD_DIM), jnp.float32)
        index = 0
        for message_ref in message_refs:
            for slot in range(message_ref.shape[0]):
                part = message_ref[slot, cols, :].astype(jnp.float32)
                carried = carried + counted_ref[index] * part
                index += 1
        state = carried.astype(jnp.bfloat16)
        from_past = jnp.dot(q_ref[:, cols], state, preferred_element_type=jnp.float32)
        out_ref[:, cols] = local_ref[:, cols] + jnp.where(joined, from_past, 0.0)


def head_specs(count, heads, parts):
    return [pl.BlockSpec((count, heads * HEAD_DIM), lambda b, p=p: (b, p)) for p in parts]


def doc_specs(count):
    return [
        pl.BlockSpec((None, count, 1), lambda b: (b, 0, 0)),
        pl.BlockSpec((None, 1, count), lambda b: (b, 0, 0)),
    ]


def state_spec(heads):
    return pl.BlockSpec((None, heads, HEAD_DIM, HEAD_DIM), lambda b: (b, 0, 0, 0))


def local_attention(qkv, docs, heads):
    blocks, count = docs.shape
    return pl.pallas_call(
        _local_kernel,
        grid=(blocks,),
        in_specs=head_specs(count, heads, (0, 1, 2)) + doc_specs(count),
        out_specs=head_specs(count, heads, (0,))[0],
        out_shape=jax.ShapeDtypeStruct((blocks * count, heads * HEAD_DIM), jnp.float32),
    )(qkv, qkv, qkv, docs.reshape(blocks, count, 1), docs.reshape(blocks, 1, count))


def tail_states(qkv, docs, heads):
    blocks, count = docs.shape
    width = heads * HEAD_DIM
    return pl.pallas_call(
        _tail_kernel,
        grid=(1,),
        in_specs=[
            pl.BlockSpec((blocks * count, width), lambda i: (0, 1)),
            pl.BlockSpec((blocks * count, width), lambda i: (0, 2)),
            pl.BlockSpec((blocks, count, 1), lambda i: (0, 0, 0)),
            pl.BlockSpec((blocks, 1, count), lambda i: (0, 0, 0)),
        ],
        out_specs=[
            pl.BlockSpec((blocks, width, HEAD_DIM), lambda i: (0, 0, 0)),
            pl.BlockSpec((1, width + 16, HEAD_DIM), lambda i: (0, 0, 0)),
        ],
        out_shape=[
            jax.ShapeDtypeStruct((blocks, width, HEAD_DIM), jnp.bfloat16),
            jax.ShapeDtypeStruct((1, width + 16, HEAD_DIM), jnp.bfloat16),
        ],
    )(qkv, qkv, docs.reshape(blocks, count, 1), docs.reshape(blocks, 1, count))


def add_past(local, qkv, counted, messages, docs, heads):
    blocks, count = docs.shape
    tile = head_specs(count, heads, (0,))[0]
    sources = counted.shape[1]
    whole = [pl.BlockSpec(message.shape, lambda b: (0, 0, 0)) for message in messages]
    return pl.pallas_call(
        _past_kernel,
        grid=(blocks,),
        in_specs=[tile, tile, pl.BlockSpec((None, sources, 1, HEAD_DIM), lambda b: (b, 0, 0, 0))]
        + doc_specs(count)
        + whole,
        out_specs=tile,
        out_shape=jax.ShapeDtypeStruct(local.shape, jnp.float32),
        input_output_aliases={0: 0},
    )(local, qkv, counted, docs.reshape(blocks, count, 1), docs.reshape(blocks, 1, count), *messages)


def make_shards(n_sq, n_fsdp):
    def shards(tokens, doc_ids, norm_gain, query_weight, key_weight, value_weight, out_gain):
        core = lax.axis_index("core")
        sq = lax.axis_index("sq")
        count, width = tokens.shape[1], tokens.shape[2]
        rows = query_weight.shape[0]
        half = ATTN_WIDTH // 2
        heads = HEADS // 2

        normed = norm_rows(tokens[0].astype(jnp.float32), norm_gain).astype(jnp.bfloat16)
        normed = normed.reshape(count, n_sq, 2, n_fsdp, rows).transpose(0, 1, 3, 2, 4)
        normed = normed.reshape(count, width)
        pair = jnp.concatenate([normed, swap_core(normed)], axis=0)

        own_docs = doc_ids[0]
        docs = jnp.stack([own_docs, swap_core(own_docs)])
        first, last = docs[:, 0], docs[:, -1]

        def halves(start):
            return jnp.concatenate(
                [
                    lax.dynamic_slice_in_dim(weight, start, half, axis=1)
                    for weight in (query_weight, key_weight, value_weight)
                ],
                axis=1,
            )

        mine, other = halves(core * half), halves((1 - core) * half)
        both = in_core_order(core, mine, swap_core(other))
        gathered = lax.all_gather(both, ("sq", "fsdp"), axis=0, tiled=False)
        summed = jnp.dot(pair, gathered.reshape(width, 3 * half), preferred_element_type=jnp.float32)
        qkv = jax.nn.silu(summed).astype(jnp.bfloat16)

        slot_core = jnp.stack([core, 1 - core])
        block = 2 * sq + slot_core

        own_message, message = tail_states(qkv, docs, heads)
        local_part = local_attention(qkv, docs, heads)

        own_counted = (block[None, :] < block[:, None]) & (last[None, :] == first[:, None])
        received = lax.all_to_all(
            jnp.broadcast_to(message, (n_sq,) + message.shape[1:]), "sq", 0, 0, tiled=True
        )
        chip_last = received[:, heads * HEAD_DIM, 0].astype(jnp.int32)
        sources = jnp.arange(n_sq, dtype=jnp.int32)
        far_counted = (sources < sq)[None, :] & (chip_last[None, :] == first[:, None])
        counted = jnp.concatenate([own_counted, far_counted], axis=1)
        counted = jnp.broadcast_to(
            counted.reshape(2, n_sq + 2, 1, 1).astype(jnp.float32), (2, n_sq + 2, 1, HEAD_DIM)
        )

        mixed = add_past(local_part, qkv, counted, [own_message, received], docs, heads)
        mixed = mixed.reshape(2, count, half)
        squares = jnp.sum(mixed * mixed, axis=-1)
        total = squares + swap_core(squares)[::-1]
        scale = lax.rsqrt(total / ATTN_WIDTH + EPS)
        gain = lax.dynamic_slice_in_dim(out_gain, core * half, half)
        attended = (mixed * scale[:, :, None] * gain).astype(jnp.bfloat16)
        theirs = swap_core(attended[1])
        out = jnp.where(
            core == 0,
            jnp.concatenate([attended[0], theirs], axis=-1),
            jnp.concatenate([theirs, attended[0]], axis=-1),
        )
        return out[None]

    return shards


def solution(mesh):
    n_seq, n_fsdp = mesh.shape["seq"], mesh.shape["fsdp"]
    chips = Mesh(mesh.devices.reshape(n_seq // 2, 2, n_fsdp), ("sq", "core", "fsdp"))
    seq = ("sq", "core")
    in_specs = (
        P("fsdp", seq, None),
        P("fsdp", seq),
        P(),
        P(("sq", "core", "fsdp"), None),
        P(("sq", "core", "fsdp"), None),
        P(("sq", "core", "fsdp"), None),
        P(),
    )
    out_specs = P("fsdp", seq, None)
    return jax.shard_map(
        make_shards(n_seq // 2, n_fsdp), mesh=chips, in_specs=in_specs, out_specs=out_specs, check_vma=False
    )
```

```python
import jax
import jax.numpy as jnp
from jax import lax
from jax.sharding import Mesh, PartitionSpec as P
from jax.experimental import pallas as pl

HEADS = 12
HEAD_DIM = 128
ATTN_WIDTH = 1536


EPS = 1e-06


def norm_rows(values, gain):
    mean_sq = jnp.mean(values * values, axis=-1, keepdims=True)
    return values * lax.rsqrt(mean_sq + EPS) * gain


def swap_core(value):
    return lax.ppermute(value, "core", [(0, 1), (1, 0)])


def in_core_order(core, mine, theirs):
    return jnp.where(core == 0, jnp.stack([mine, theirs]), jnp.stack([theirs, mine]))


def head_columns(ref):
    return [slice(h * HEAD_DIM, (h + 1) * HEAD_DIM) for h in range(ref.shape[1] // HEAD_DIM)]


def _local_kernel(q_ref, k_ref, v_ref, dcol_ref, drow_ref, local_ref):
    count = q_ref.shape[0]
    row_pos = lax.broadcasted_iota(jnp.int32, (count, count), 0)
    col_pos = lax.broadcasted_iota(jnp.int32, (count, count), 1)
    visible = (row_pos >= col_pos) & (dcol_ref[...] == drow_ref[...])
    for cols in head_columns(q_ref):
        scores = lax.dot_general(
            q_ref[:, cols], k_ref[:, cols], (((1,), (1,)), ((), ())), preferred_element_type=jnp.float32
        )
        weights = jnp.where(visible, scores, 0.0).astype(jnp.bfloat16)
        local_ref[:, cols] = jnp.dot(weights, v_ref[:, cols], preferred_element_type=jnp.float32)


def _tail_kernel(k_ref, v_ref, dcol_ref, drow_ref, own_ref, message_ref):
    count = dcol_ref.shape[1]
    lasts = [drow_ref[block][:, count - 1:count] for block in range(2)]
    chip_last = jnp.maximum(lasts[0], lasts[1])
    for h, cols in enumerate(head_columns(k_ref)):
        chip = jnp.zeros((HEAD_DIM, HEAD_DIM), jnp.float32)
        for block in range(2):
            rows = slice(block * count, (block + 1) * count)
            ending = dcol_ref[block] == lasts[block]
            tail_keys = jnp.where(ending, k_ref[rows, cols], jnp.zeros((count, HEAD_DIM), k_ref.dtype))
            tail = lax.dot_general(
                tail_keys, v_ref[rows, cols], (((0,), (0,)), ((), ())), preferred_element_type=jnp.float32
            )
            own_ref[block, cols, :] = tail.astype(jnp.bfloat16)
            chip = chip + jnp.where(lasts[block] == chip_last, tail, 0.0)
        message_ref[0, cols, :] = chip.astype(jnp.bfloat16)
    tag = jnp.broadcast_to(chip_last.astype(jnp.float32), (16, HEAD_DIM)).astype(jnp.bfloat16)
    message_ref[0, pl.ds(k_ref.shape[1], 16), :] = tag


def _past_kernel(local_ref, q_ref, counted_ref, dcol_ref, drow_ref, *rest):
    message_refs, out_ref = rest[:-1], rest[-1]
    joined = dcol_ref[...] == drow_ref[...][:, 0:1]
    for h, cols in enumerate(head_columns(q_ref)):
        carried = jnp.zeros((HEAD_DIM, HEAD_DIM), jnp.float32)
        index = 0
        for message_ref in message_refs:
            for slot in range(message_ref.shape[0]):
                part = message_ref[slot, cols, :].astype(jnp.float32)
                carried = carried + counted_ref[index] * part
                index += 1
        state = carried.astype(jnp.bfloat16)
        from_past = jnp.dot(q_ref[:, cols], state, preferred_element_type=jnp.float32)
        out_ref[:, cols] = local_ref[:, cols] + jnp.where(joined, from_past, 0.0)


def head_specs(count, heads, parts):
    return [pl.BlockSpec((count, heads * HEAD_DIM), lambda b, p=p: (b, p)) for p in parts]


def doc_specs(count):
    return [
        pl.BlockSpec((None, count, 1), lambda b: (b, 0, 0)),
        pl.BlockSpec((None, 1, count), lambda b: (b, 0, 0)),
    ]


def state_spec(heads):
    return pl.BlockSpec((None, heads, HEAD_DIM, HEAD_DIM), lambda b: (b, 0, 0, 0))


def local_attention(qkv, docs, heads):
    blocks, count = docs.shape
    return pl.pallas_call(
        _local_kernel,
        grid=(blocks,),
        in_specs=head_specs(count, heads, (0, 1, 2)) + doc_specs(count),
        out_specs=head_specs(count, heads, (0,))[0],
        out_shape=jax.ShapeDtypeStruct((blocks * count, heads * HEAD_DIM), jnp.float32),
    )(qkv, qkv, qkv, docs.reshape(blocks, count, 1), docs.reshape(blocks, 1, count))


def tail_states(qkv, docs, heads):
    blocks, count = docs.shape
    width = heads * HEAD_DIM
    return pl.pallas_call(
        _tail_kernel,
        grid=(1,),
        in_specs=[
            pl.BlockSpec((blocks * count, width), lambda i: (0, 1)),
            pl.BlockSpec((blocks * count, width), lambda i: (0, 2)),
            pl.BlockSpec((blocks, count, 1), lambda i: (0, 0, 0)),
            pl.BlockSpec((blocks, 1, count), lambda i: (0, 0, 0)),
        ],
        out_specs=[
            pl.BlockSpec((blocks, width, HEAD_DIM), lambda i: (0, 0, 0)),
            pl.BlockSpec((1, width + 16, HEAD_DIM), lambda i: (0, 0, 0)),
        ],
        out_shape=[
            jax.ShapeDtypeStruct((blocks, width, HEAD_DIM), jnp.bfloat16),
            jax.ShapeDtypeStruct((1, width + 16, HEAD_DIM), jnp.bfloat16),
        ],
    )(qkv, qkv, docs.reshape(blocks, count, 1), docs.reshape(blocks, 1, count))


def add_past(local, qkv, counted, messages, docs, heads):
    blocks, count = docs.shape
    tile = head_specs(count, heads, (0,))[0]
    sources = counted.shape[1]
    whole = [pl.BlockSpec(message.shape, lambda b: (0, 0, 0)) for message in messages]
    return pl.pallas_call(
        _past_kernel,
        grid=(blocks,),
        in_specs=[tile, tile, pl.BlockSpec((None, sources, 1, HEAD_DIM), lambda b: (b, 0, 0, 0))]
        + doc_specs(count)
        + whole,
        out_specs=tile,
        out_shape=jax.ShapeDtypeStruct(local.shape, jnp.float32),
        input_output_aliases={0: 0},
    )(local, qkv, counted, docs.reshape(blocks, count, 1), docs.reshape(blocks, 1, count), *messages)


def make_shards(n_sq, n_fsdp):
    def shards(tokens, doc_ids, norm_gain, query_weight, key_weight, value_weight, out_gain):
        core = lax.axis_index("core")
        sq = lax.axis_index("sq")
        count, width = tokens.shape[1], tokens.shape[2]
        rows = query_weight.shape[0]
        half = ATTN_WIDTH // 2
        heads = HEADS // 2

        normed = norm_rows(tokens[0].astype(jnp.float32), norm_gain).astype(jnp.bfloat16)
        normed = normed.reshape(count, n_sq, 2, n_fsdp, rows).transpose(0, 1, 3, 2, 4)
        normed = normed.reshape(count, width)
        pair = jnp.concatenate([normed, swap_core(normed)], axis=0)

        own_docs = doc_ids[0]
        docs = jnp.stack([own_docs, swap_core(own_docs)])
        first, last = docs[:, 0], docs[:, -1]
        chip_last = jnp.stack(
            [
                lax.ppermute(jnp.max(last), "sq", [(i, i + shift) for i in range(n_sq - shift)])
                for shift in range(1, n_sq)
            ]
        )
        flipped = pair.reshape(2 * count, n_sq, n_fsdp, 2, rows)[:, :, :, ::-1].reshape(2 * count, width)
        pair = jnp.where(core == 0, pair, flipped)
        slot_core = jnp.stack([core, 1 - core])
        block = 2 * sq + slot_core
        own_counted = (block[None, :] < block[:, None]) & (last[None, :] == first[:, None])
        far_counted = (jnp.arange(1, n_sq, dtype=jnp.int32) <= sq)[None, :] & (chip_last[None, :] == first[:, None])
        counted = jnp.concatenate([own_counted, far_counted], axis=1)
        counted = jnp.broadcast_to(
            counted.reshape(2, n_sq + 1, 1, 1).astype(jnp.float32), (2, n_sq + 1, 1, HEAD_DIM)
        )
        pair, counted = lax.optimization_barrier((pair, counted))

        def halves(start):
            return jnp.concatenate(
                [
                    lax.dynamic_slice_in_dim(weight, start, half, axis=1)
                    for weight in (query_weight, key_weight, value_weight)
                ],
                axis=1,
            )

        mine, other = halves(core * half), halves((1 - core) * half)
        both = jnp.stack([mine, swap_core(other)])
        gathered = lax.all_gather(both, ("sq", "fsdp"), axis=0, tiled=False)
        summed = jnp.dot(pair, gathered.reshape(width, 3 * half), preferred_element_type=jnp.float32)
        qkv = jax.nn.silu(summed).astype(jnp.bfloat16)

        slot_core = jnp.stack([core, 1 - core])
        block = 2 * sq + slot_core

        own_message, message = tail_states(qkv, docs, heads)
        local_part = local_attention(qkv, docs, heads)

        received = [
            lax.ppermute(message, "sq", [(i, i + shift) for i in range(n_sq - shift)])
            for shift in range(1, n_sq)
        ]

        mixed = add_past(local_part, qkv, counted, [own_message] + received, docs, heads)
        mixed = mixed.reshape(2, count, half)
        squares = jnp.sum(mixed * mixed, axis=-1)
        total = squares + swap_core(squares)[::-1]
        scale = lax.rsqrt(total / ATTN_WIDTH + EPS)
        gain = lax.dynamic_slice_in_dim(out_gain, core * half, half)
        attended = (mixed * scale[:, :, None] * gain).astype(jnp.bfloat16)
        theirs = swap_core(attended[1])
        out = jnp.where(
            core == 0,
            jnp.concatenate([attended[0], theirs], axis=-1),
            jnp.concatenate([theirs, attended[0]], axis=-1),
        )
        return out[None]

    return shards


def solution(mesh):
    n_seq, n_fsdp = mesh.shape["seq"], mesh.shape["fsdp"]
    chips = Mesh(mesh.devices.reshape(n_seq // 2, 2, n_fsdp), ("sq", "core", "fsdp"))
    seq = ("sq", "core")
    in_specs = (
        P("fsdp", seq, None),
        P("fsdp", seq),
        P(),
        P(("sq", "core", "fsdp"), None),
        P(("sq", "core", "fsdp"), None),
        P(("sq", "core", "fsdp"), None),
        P(),
    )
    out_specs = P("fsdp", seq, None)
    return jax.shard_map(
        make_shards(n_seq // 2, n_fsdp), mesh=chips, in_specs=in_specs, out_specs=out_specs, check_vma=False
    )
```
